128 devices in a mesh: cube: 2 (over y_hi), front: 16 (over y_lo, x, core), col: 4 (over z).
Axes of the slice: x: 4, y: 4 (y_hi: 2, y_lo: 2; y = y_hi * 2 + y_lo), z: 4, core: 2. Of those that a mesh axis runs over, the one named last changes fastest.
Arguments:
- parent_front: float32 [8192, 8192], P(('cube', 'front'), 'col'), may hold values from -16 to 18, as said below
- child_blocks: bfloat16 [2, 6144, 6144], P('cube', 'front'), may hold values from -16 to 16, as said below
- row_maps: int32 [2, 6144], replicated, may hold values from 0 to 8191, as said below
- front_size: int32 [1], replicated, may hold values from 6144 to 8192
Outputs:
- factor: float32 [8192, 512], P(('cube', 'front'))
- schur: float32 [8192, 8192], P(('cube', 'front'), 'col')
The draws below stay inside these ranges and needn't reach their ends.
Inputs may be any that keep to these rules, and one draw needn't show every extreme that they name: `parent_front`: symmetric, and the assembled front is positive definite. `child_blocks`: each child's block is symmetric. For each child c and index i, with g = i // 192, row_maps[c, i] lies in the front rows b * 256 to (b + 1) * 256 - 1, where b = (g % 2) * 16 + g // 2; one child's entries are distinct and rise within each run of 192.
All inputs are finite; a program needn't handle non-finite values.
Results may differ from the reference program's by a relative error of at most 0.0003.
Values may be sent and summed in bfloat16 or wider, within the bound.
No kernel may reach another device: no remote copies, remote signals or barrier semaphores. Data moves between devices by JAX's collectives and lax.ppermute only.
A program may use at most 64 MiB of HBM per device.

```python
import jax
import jax.numpy as jnp
from jax import lax

F = 8192
M = 6144
PW = 256
NP = 2
K = 512
GROUPS = 32


def draw_parent_front(key, part):
    first_key, second_key = jax.random.split(key)
    inner_rank = F // 32
    factors = jnp.clip(jax.random.normal(first_key, (F, inner_rank), jnp.float32), -4.0, 4.0)
    product = jnp.dot(factors, factors.T, precision=lax.Precision.HIGHEST) / inner_rank
    symmetric = (product + product.T) * 0.5
    diagonal = jax.random.uniform(second_key, (F,), jnp.float32, 0.5, 2.0)
    identity = jnp.arange(F)[:, None] == jnp.arange(F)[None, :]
    return symmetric + jnp.where(identity, diagonal[:, None], 0.0)


def draw_child_blocks(key, part):
    inner_rank = M // 32
    factors = jnp.clip(jax.random.normal(key, (2, M, inner_rank), jnp.float32), -4.0, 4.0)
    product = jnp.einsum('cir,cjr->cij', factors, factors, precision=lax.Precision.HIGHEST) / inner_rank
    symmetric = (product + jnp.swapaxes(product, 1, 2)) * 0.5
    return symmetric.astype(jnp.bfloat16)


def draw_row_maps(key, part):
    row_block = F // GROUPS
    run_length = M // GROUPS
    keys = jax.random.split(jax.random.fold_in(key, 7), 2 * GROUPS)
    shuffled = jax.vmap(lambda single: jax.random.permutation(single, row_block))(keys)
    picked = jnp.sort(shuffled[:, :run_length].astype(jnp.int32), axis=1)
    picked = picked.reshape(2, GROUPS, run_length)
    groups_ids = jnp.arange(GROUPS, dtype=jnp.int32)
    blocks = groups_ids % 2 * (GROUPS // 2) + groups_ids // 2
    mapped = picked + (blocks * row_block)[None, :, None]
    return mapped.reshape(2, M).astype(jnp.int32)


def setup_inputs(seed: int = 0) -> dict:
    key_of = jax.random.split(jax.random.key(seed), 5)
    parent_front = draw_parent_front(jax.random.fold_in(key_of[4], 71), 0)
    child_blocks = draw_child_blocks(jax.random.fold_in(key_of[4], 71), 0)
    row_maps = draw_row_maps(jax.random.fold_in(key_of[4], 71), 0)
    front_size = jax.random.randint(key_of[3], (1,), F - F // 4, F + 1).astype(jnp.int32)
    return dict(parent_front=parent_front, child_blocks=child_blocks, row_maps=row_maps, front_size=front_size)


def reference(parent_front, child_blocks, row_maps, front_size):
    index_all = jnp.arange(F, dtype=jnp.int32)
    live = (index_all < front_size[0]).astype(jnp.float32)
    matrix = parent_front
    for child in range(2):
        mapping = row_maps[child]
        matrix = matrix.at[mapping[:, None], mapping[None, :]].add(child_blocks[child].astype(jnp.float32))
    matrix = matrix * live[:, None] * live[None, :]
    matrix = matrix + jnp.diag(1.0 - live)
    panels = []
    for index in range(NP):
        lower = index * PW
        diag_factor = jnp.linalg.cholesky(matrix[lower:lower + PW, lower:lower + PW])
        panel = lax.linalg.triangular_solve(diag_factor, matrix[:, lower:lower + PW], left_side=False, lower=True, transpose_a=True)
        panel = jnp.where((index_all >= lower)[:, None], panel, 0.0)
        matrix = matrix - jnp.dot(panel, panel.T, precision=lax.Precision.HIGHEST)
        panels.append(panel)
    factor = jnp.concatenate(panels, axis=1)
    keep = index_all >= K
    schur = jnp.where(keep[:, None] & keep[None, :], matrix, 0.0)
    return (factor, schur)
```

```python
import jax
import jax.numpy as jnp
from jax import lax
from jax.sharding import PartitionSpec as P

PW = 256
NP = 2
K = 512

HI = lax.Precision.HIGHEST


def swapped(shard, axis, distance):
    return lax.ppermute(shard, axis, [(i, i ^ 1 << distance) for i in range(lax.axis_size(axis))])


def spread(block, axis, owner):
    block = jnp.where(lax.axis_index(axis) == owner, block, jnp.zeros_like(block))
    return lax.psum(block, axis)


def pick_columns(block, col, nb, grp):
    n = block.shape[0]
    halves = block.shape[-1] // (2 * grp)
    shaped = block.reshape(n, halves, 2, grp)
    start = (col * nb) % halves
    parity = (col * nb) // halves
    shaped = lax.dynamic_slice_in_dim(shaped, start, nb, 1)
    shaped = lax.dynamic_index_in_dim(shaped, parity, 2, keepdims=False)
    return shaped


def extend(part, row_local, col_local, rows, blk):
    n, nb, grp = part.shape
    pr = (jnp.arange(rows, dtype=jnp.int32)[:, None] == row_local[None, :]).astype(part.dtype)
    pc = (col_local[:, :, None] == jnp.arange(blk, dtype=jnp.int32)[None, None, :]).astype(part.dtype)
    placed_rows = jnp.dot(pr, part.reshape(n, nb * grp), preferred_element_type=jnp.float32)
    placed_rows = placed_rows.astype(part.dtype).reshape(rows, nb, grp)
    placed = jnp.einsum("ija,jab->ijb", placed_rows, pc, preferred_element_type=jnp.float32)
    return placed.reshape(rows, nb * blk)


def shards(parent_front, child_blocks, row_maps, front_size):
    rows, width = parent_front.shape
    half = child_blocks.shape[1] // 2
    grp = half
    blk = rows
    nb = width // blk
    side = lax.axis_index("cube")
    front_pos = lax.axis_index("front")
    col = lax.axis_index("col")
    row_block = lax.axis_index(("cube", "front"))
    row_start = row_block * rows
    col_start = col * width
    row_ids = row_start + jnp.arange(rows, dtype=jnp.int32)
    col_ids = col_start + jnp.arange(width, dtype=jnp.int32)

    own_map = lax.dynamic_index_in_dim(row_maps, side, 0, keepdims=False)
    other_map = lax.dynamic_index_in_dim(row_maps, 1 - side, 0, keepdims=False)
    first = front_pos * 2 * half + side * half
    own_rows = lax.dynamic_slice_in_dim(own_map, first, half) - row_start
    other_rows = lax.dynamic_slice_in_dim(other_map, first, half) - row_start
    blk_starts = col_start + blk * jnp.arange(nb, dtype=jnp.int32)[:, None]
    own_cols = pick_columns(own_map[None], col, nb, grp)[0] - blk_starts
    other_cols = pick_columns(other_map[None], col, nb, grp)[0] - blk_starts

    local_block = child_blocks[0]
    kept_rows = lax.dynamic_slice_in_dim(local_block, side * half, half, 0)
    sent_rows = lax.dynamic_slice_in_dim(local_block, (1 - side) * half, half, 0)
    kept = pick_columns(kept_rows, col, nb, grp)
    sent = pick_columns(sent_rows, col, nb, grp)
    arrived = swapped(sent, "cube", 0)
    own_part = extend(kept, own_rows, own_cols, rows, blk)
    other_part = extend(arrived, other_rows, other_cols, rows, blk)
    first_child = jnp.where(side == 0, own_part, other_part)
    second_child = jnp.where(side == 0, other_part, own_part)
    matrix = parent_front + first_child
    matrix = matrix + second_child

    live_rows = row_ids < front_size[0]
    live_cols = col_ids < front_size[0]
    matrix = jnp.where(live_rows[:, None] & live_cols[None, :], matrix, 0.0)
    matrix = matrix + jnp.where(
        (row_ids[:, None] == col_ids[None, :]) & jnp.logical_not(live_rows)[:, None], 1.0, 0.0
    )

    pcols = NP * PW
    nd = pcols // rows
    head_local = matrix[:, :pcols]
    own = spread(head_local, "col", 0)
    top_parts = jnp.where(
        (jnp.arange(nd)[:, None, None] == row_block) & (col == 0), head_local[None], 0.0
    )
    top = lax.psum(top_parts, ("cube", "front", "col")).reshape(pcols, pcols)
    top_ids = jnp.arange(pcols, dtype=jnp.int32)

    panels = []
    for index in range(NP):
        lower = index * PW
        diag_factor = jnp.linalg.cholesky(top[lower : lower + PW, lower : lower + PW])
        both = jnp.concatenate([top[:, lower : lower + PW], own[:, lower : lower + PW]], 0)
        solved = lax.linalg.triangular_solve(
            diag_factor, both, left_side=False, lower=True, transpose_a=True
        )
        top_panel = jnp.where((top_ids >= lower)[:, None], solved[:pcols], 0.0)
        panel = jnp.where((row_ids >= lower)[:, None], solved[pcols:], 0.0)
        if index + 1 < NP:
            top = top - jnp.dot(top_panel, top_panel.T, precision=HI)
            own = own - jnp.dot(panel, top_panel.T, precision=HI)
        panels.append(panel)
    factor = jnp.concatenate(panels, axis=1)

    gathered = lax.all_gather(factor, ("cube", "front"), tiled=True)
    col_factor = lax.dynamic_slice_in_dim(gathered, col_start, width, 0)
    update = lax.dot_general(
        factor, col_factor, (((1,), (1,)), ((), ())), precision=HI
    )
    matrix = matrix - update
    keep_rows = row_ids >= K
    keep_cols = col_ids >= K
    schur = jnp.where(keep_rows[:, None] & keep_cols[None, :], matrix, 0.0)
    return (factor, schur)


def solution(mesh):
    in_specs = (P(("cube", "front"), "col"), P("cube", "front", None), P(), P())
    out_specs = (P(("cube", "front"), None), P(("cube", "front"), "col"))
    return jax.shard_map(shards, mesh=mesh, in_specs=in_specs, out_specs=out_specs, check_vma=False)
```

```python
import jax
import jax.numpy as jnp
from jax import lax
from jax.sharding import PartitionSpec as P

PW = 256
NP = 2
K = 512

HI = lax.Precision.HIGHEST


def swapped(shard, axis, distance):
    return lax.ppermute(shard, axis, [(i, i ^ 1 << distance) for i in range(lax.axis_size(axis))])


def spread(block, axis, owner):
    block = jnp.where(lax.axis_index(axis) == owner, block, jnp.zeros_like(block))
    return lax.psum(block, axis)


def pick_columns(block, col, nb, grp):
    n = block.shape[0]
    halves = block.shape[-1] // (2 * grp)
    shaped = block.reshape(n, halves, 2, grp)
    start = (col * nb) % halves
    parity = (col * nb) // halves
    shaped = lax.dynamic_slice_in_dim(shaped, start, nb, 1)
    shaped = lax.dynamic_index_in_dim(shaped, parity, 2, keepdims=False)
    return shaped


def extend(part, row_local, col_local, rows, blk):
    n, nb, grp = part.shape
    pr = (jnp.arange(rows, dtype=jnp.int32)[:, None] == row_local[None, :]).astype(part.dtype)
    pc = (col_local[:, :, None] == jnp.arange(blk, dtype=jnp.int32)[None, None, :]).astype(part.dtype)
    placed_rows = jnp.dot(pr, part.reshape(n, nb * grp), preferred_element_type=jnp.float32)
    placed_rows = placed_rows.astype(part.dtype).reshape(rows, nb, grp)
    placed = jnp.einsum("ija,jab->ijb", placed_rows, pc, preferred_element_type=jnp.float32)
    return placed.reshape(rows, nb * blk)


def shards(parent_front, child_blocks, row_maps, front_size):
    rows, width = parent_front.shape
    half = child_blocks.shape[1] // 2
    grp = half
    blk = rows
    nb = width // blk
    side = lax.axis_index("cube")
    front_pos = lax.axis_index("front")
    col = lax.axis_index("col")
    row_block = lax.axis_index(("cube", "front"))
    row_start = row_block * rows
    col_start = col * width
    row_ids = row_start + jnp.arange(rows, dtype=jnp.int32)
    col_ids = col_start + jnp.arange(width, dtype=jnp.int32)

    own_map = lax.dynamic_index_in_dim(row_maps, side, 0, keepdims=False)
    other_map = lax.dynamic_index_in_dim(row_maps, 1 - side, 0, keepdims=False)
    first = front_pos * 2 * half + side * half
    own_rows = lax.dynamic_slice_in_dim(own_map, first, half) - row_start
    other_rows = lax.dynamic_slice_in_dim(other_map, first, half) - row_start
    blk_starts = col_start + blk * jnp.arange(nb, dtype=jnp.int32)[:, None]
    own_cols = pick_columns(own_map[None], col, nb, grp)[0] - blk_starts
    other_cols = pick_columns(other_map[None], col, nb, grp)[0] - blk_starts

    local_block = child_blocks[0]
    kept_rows = lax.dynamic_slice_in_dim(local_block, side * half, half, 0)
    sent_rows = lax.dynamic_slice_in_dim(local_block, (1 - side) * half, half, 0)
    kept = pick_columns(kept_rows, col, nb, grp)
    sent = pick_columns(sent_rows, col, nb, grp)
    arrived = swapped(sent, "cube", 0)
    own_part = extend(kept, own_rows, own_cols, rows, blk)
    other_part = extend(arrived, other_rows, other_cols, rows, blk)
    first_child = jnp.where(side == 0, own_part, other_part)
    second_child = jnp.where(side == 0, other_part, own_part)
    matrix = parent_front + first_child
    matrix = matrix + second_child

    live_rows = row_ids < front_size[0]
    live_cols = col_ids < front_size[0]
    matrix = jnp.where(live_rows[:, None] & live_cols[None, :], matrix, 0.0)
    matrix = matrix + jnp.where(
        (row_ids[:, None] == col_ids[None, :]) & jnp.logical_not(live_rows)[:, None], 1.0, 0.0
    )

    pcols = NP * PW
    head_local = matrix[:, :pcols]
    ncol = lax.axis_size("col")
    arrived_heads = [
        lax.ppermute(head_local, "col", [(0, d)]) for d in range(1, ncol)
    ]
    own = head_local
    for d, piece in enumerate(arrived_heads, start=1):
        own = jnp.where(col == d, piece, own)

    everyone = ("cube", "front", "col")
    ndev = lax.axis_size(everyone)
    nd = pcols // rows
    chunk = rows * pcols // ndev
    send = jnp.concatenate(
        [
            jnp.where((row_block == b) & (col == 0), head_local, 0.0).reshape(ndev, chunk)
            for b in range(nd)
        ],
        axis=1,
    )
    scattered = lax.all_to_all(send, everyone, 0, 0, tiled=True)
    src_index = [b * ncol for b in range(nd)]
    piece = jnp.concatenate(
        [scattered[src_index[b], b * chunk : (b + 1) * chunk] for b in range(nd)]
    )
    spread_out = jnp.broadcast_to(piece[None], (ndev, nd * chunk))
    gathered_top = lax.all_to_all(spread_out, everyone, 0, 0, tiled=True)
    top = jnp.concatenate(
        [gathered_top[:, b * chunk : (b + 1) * chunk].reshape(rows, pcols) for b in range(nd)],
        axis=0,
    )
    top_ids = jnp.arange(pcols, dtype=jnp.int32)
    eye = jnp.eye(PW, dtype=jnp.float32)

    panels = []
    update = None
    for index in range(NP):
        lower = index * PW
        diag_factor = jnp.linalg.cholesky(top[lower : lower + PW, lower : lower + PW])
        inverse = lax.linalg.triangular_solve(
            diag_factor, eye, left_side=True, lower=True, transpose_a=False
        )
        both = jnp.concatenate([top[:, lower : lower + PW], own[:, lower : lower + PW]], 0)
        solved = jnp.dot(both, inverse.T, precision=HI)
        top_panel = jnp.where((top_ids >= lower)[:, None], solved[:pcols], 0.0)
        panel = jnp.where((row_ids >= lower)[:, None], solved[pcols:], 0.0)
        if index + 1 < NP:
            top = top - jnp.dot(top_panel, top_panel.T, precision=HI)
            own = own - jnp.dot(panel, top_panel.T, precision=HI)
        panels.append(panel)
        gathered = lax.all_gather(panel, ("cube", "front"), tiled=True)
        col_panel = lax.dynamic_slice_in_dim(gathered, col_start, width, 0)
        term = lax.dot_general(panel, col_panel, (((1,), (1,)), ((), ())), precision=HI)
        update = term if update is None else update + term
    factor = jnp.concatenate(panels, axis=1)
    matrix = matrix - update
    keep_rows = row_ids >= K
    keep_cols = col_ids >= K
    schur = jnp.where(keep_rows[:, None] & keep_cols[None, :], matrix, 0.0)
    return (factor, schur)


def solution(mesh):
    in_specs = (P(("cube", "front"), "col"), P("cube", "front", None), P(), P())
    out_specs = (P(("cube", "front"), None), P(("cube", "front"), "col"))
    return jax.shard_map(shards, mesh=mesh, in_specs=in_specs, out_specs=out_specs, check_vma=False)
```

```python
import jax
import jax.numpy as jnp
from jax import lax
from jax.sharding import PartitionSpec as P

PW = 256
NP = 2
K = 512

HI = lax.Precision.HIGHEST


def swapped(shard, axis, distance):
    return lax.ppermute(shard, axis, [(i, i ^ 1 << distance) for i in range(lax.axis_size(axis))])


def spread(block, axis, owner):
    block = jnp.where(lax.axis_index(axis) == owner, block, jnp.zeros_like(block))
    return lax.psum(block, axis)


def column_span(block, col, nb, grp):
    span = nb * 2 * grp
    start = (col * span) % block.shape[-1]
    return lax.dynamic_slice_in_dim(block, start, span, block.ndim - 1)


def one_hot(index, size, dtype):
    return (index[..., None] == jnp.arange(size, dtype=jnp.int32)).astype(dtype)


def place(part, row_local, col_local, rows, blk):
    nb, w = col_local.shape
    pr = one_hot(row_local, rows, part.dtype).T
    placed_rows = jnp.dot(pr, part, preferred_element_type=jnp.float32).astype(part.dtype)
    pieces = [
        jnp.dot(
            placed_rows[:, j * w : (j + 1) * w],
            one_hot(col_local[j], blk, part.dtype),
            preferred_element_type=jnp.float32,
        )
        for j in range(nb)
    ]
    return jnp.concatenate(pieces, axis=1)


def shards(parent_front, child_blocks, row_maps, front_size):
    rows, width = parent_front.shape
    half = child_blocks.shape[1] // 2
    grp = half
    blk = rows
    nb = width // blk
    side = lax.axis_index("cube")
    front_pos = lax.axis_index("front")
    col = lax.axis_index("col")
    row_block = lax.axis_index(("cube", "front"))
    row_start = row_block * rows
    col_start = col * width
    row_ids = row_start + jnp.arange(rows, dtype=jnp.int32)
    col_ids = col_start + jnp.arange(width, dtype=jnp.int32)

    own_map = lax.dynamic_index_in_dim(row_maps, side, 0, keepdims=False)
    other_map = lax.dynamic_index_in_dim(row_maps, 1 - side, 0, keepdims=False)
    first = front_pos * 2 * half + side * half
    own_rows = lax.dynamic_slice_in_dim(own_map, first, half) - row_start
    other_rows = lax.dynamic_slice_in_dim(other_map, first, half) - row_start
    blk_starts = col_start + blk * jnp.arange(nb, dtype=jnp.int32)[:, None]
    pair = 2 * grp
    parity = (col * nb * blk) // (lax.axis_size("front") * blk)
    own_cols = column_span(own_map, col, nb, grp).reshape(nb, pair) - blk_starts
    other_cols = column_span(other_map, col, nb, grp).reshape(nb, pair)
    other_cols = lax.dynamic_slice_in_dim(other_cols, parity * grp, grp, 1) - blk_starts

    local_block = child_blocks[0]
    kept_rows = lax.dynamic_slice_in_dim(local_block, side * half, half, 0)
    sent_rows = lax.dynamic_slice_in_dim(local_block, (1 - side) * half, half, 0)
    kept = column_span(kept_rows, col, nb, grp)
    sent_span = column_span(sent_rows, col, nb, grp)
    pick = one_hot(parity * grp + jnp.arange(grp, dtype=jnp.int32), pair, sent_span.dtype).T
    sent = jnp.concatenate(
        [
            jnp.dot(sent_span[:, j * pair : (j + 1) * pair], pick, preferred_element_type=jnp.float32)
            for j in range(nb)
        ],
        axis=1,
    ).astype(sent_span.dtype)
    arrived = swapped(sent, "cube", 0)
    own_part = place(kept, own_rows, own_cols, rows, blk)
    other_part = place(arrived, other_rows, other_cols, rows, blk)
    first_child = jnp.where(side == 0, own_part, other_part)
    second_child = jnp.where(side == 0, other_part, own_part)
    matrix = parent_front + first_child
    matrix = matrix + second_child

    live_rows = row_ids < front_size[0]
    live_cols = col_ids < front_size[0]
    matrix = jnp.where(live_rows[:, None] & live_cols[None, :], matrix, 0.0)
    matrix = matrix + jnp.where(
        (row_ids[:, None] == col_ids[None, :]) & jnp.logical_not(live_rows)[:, None], 1.0, 0.0
    )

    pcols = NP * PW
    head_local = matrix[:, :pcols]
    ncol = lax.axis_size("col")
    arrived_heads = [
        lax.ppermute(head_local, "col", [(0, d)]) for d in range(1, ncol)
    ]
    own = head_local
    for d, piece in enumerate(arrived_heads, start=1):
        own = jnp.where(col == d, piece, own)

    everyone = ("cube", "front", "col")
    ndev = lax.axis_size(everyone)
    nd = pcols // rows
    chunk = rows * pcols // ndev
    send = jnp.concatenate(
        [
            jnp.where((row_block == b) & (col == 0), head_local, 0.0).reshape(ndev, chunk)
            for b in range(nd)
        ],
        axis=1,
    )
    scattered = lax.all_to_all(send, everyone, 0, 0, tiled=True)
    src_index = [b * ncol for b in range(nd)]
    piece = jnp.concatenate(
        [scattered[src_index[b], b * chunk : (b + 1) * chunk] for b in range(nd)]
    )
    spread_out = jnp.broadcast_to(piece[None], (ndev, nd * chunk))
    gathered_top = lax.all_to_all(spread_out, everyone, 0, 0, tiled=True)
    top = jnp.concatenate(
        [gathered_top[:, b * chunk : (b + 1) * chunk].reshape(rows, pcols) for b in range(nd)],
        axis=0,
    )
    top_ids = jnp.arange(pcols, dtype=jnp.int32)
    eye = jnp.eye(PW, dtype=jnp.float32)

    col_head = lax.dynamic_slice_in_dim(
        lax.all_gather(own, ("cube", "front"), tiled=True), col_start, width, 0
    )

    panels = []
    col_panels = []
    for index in range(NP):
        lower = index * PW
        diag_factor = jnp.linalg.cholesky(top[lower : lower + PW, lower : lower + PW])
        inverse = lax.linalg.triangular_solve(
            diag_factor, eye, left_side=True, lower=True, transpose_a=False
        )
        both = jnp.concatenate([top[:, lower : lower + PW], own[:, lower : lower + PW]], 0)
        solved = jnp.dot(both, inverse.T, precision=HI)
        top_panel = jnp.where((top_ids >= lower)[:, None], solved[:pcols], 0.0)
        panel = jnp.where((row_ids >= lower)[:, None], solved[pcols:], 0.0)
        col_panel = jnp.dot(col_head[:, lower : lower + PW], inverse.T, precision=HI)
        col_panel = jnp.where((col_ids >= lower)[:, None], col_panel, 0.0)
        if index + 1 < NP:
            top = top - jnp.dot(top_panel, top_panel.T, precision=HI)
            own = own - jnp.dot(panel, top_panel.T, precision=HI)
            col_head = col_head - jnp.dot(col_panel, top_panel.T, precision=HI)
        panels.append(panel)
        col_panels.append(col_panel)
    factor = jnp.concatenate(panels, axis=1)
    col_factor = jnp.concatenate(col_panels, axis=1)
    update = lax.dot_general(factor, col_factor, (((1,), (1,)), ((), ())), precision=HI)
    matrix = matrix - update
    keep_rows = row_ids >= K
    keep_cols = col_ids >= K
    schur = jnp.where(keep_rows[:, None] & keep_cols[None, :], matrix, 0.0)
    return (factor, schur)


def solution(mesh):
    in_specs = (P(("cube", "front"), "col"), P("cube", "front", None), P(), P())
    out_specs = (P(("cube", "front"), None), P(("cube", "front"), "col"))
    return jax.shard_map(shards, mesh=mesh, in_specs=in_specs, out_specs=out_specs, check_vma=False)
```

```python
import jax
import jax.numpy as jnp
from jax import lax
from jax.sharding import PartitionSpec as P

PW = 256
NP = 2
K = 512

HI = lax.Precision.HIGHEST


def swapped(shard, axis, distance):
    return lax.ppermute(shard, axis, [(i, i ^ 1 << distance) for i in range(lax.axis_size(axis))])


def spread(block, axis, owner):
    block = jnp.where(lax.axis_index(axis) == owner, block, jnp.zeros_like(block))
    return lax.psum(block, axis)


def column_span(block, col, nb, grp):
    span = nb * 2 * grp
    start = (col * span) % block.shape[-1]
    return lax.dynamic_slice_in_dim(block, start, span, block.ndim - 1)


def one_hot(index, size, dtype):
    return (index[..., None] == jnp.arange(size, dtype=jnp.int32)).astype(dtype)


def place(part, row_local, col_local, rows, blk):
    nb, w = col_local.shape
    pr = one_hot(row_local, rows, part.dtype).T
    placed_rows = jnp.dot(pr, part, preferred_element_type=jnp.float32).astype(part.dtype)
    pieces = [
        jnp.dot(
            placed_rows[:, j * w : (j + 1) * w],
            one_hot(col_local[j], blk, part.dtype),
            preferred_element_type=jnp.float32,
        )
        for j in range(nb)
    ]
    return jnp.concatenate(pieces, axis=1)


def shards(parent_front, child_blocks, row_maps, front_size):
    rows, width = parent_front.shape
    half = child_blocks.shape[1] // 2
    grp = half
    blk = rows
    nb = width // blk
    side = lax.axis_index("cube")
    front_pos = lax.axis_index("front")
    col = lax.axis_index("col")
    row_block = lax.axis_index(("cube", "front"))
    row_start = row_block * rows
    col_start = col * width
    row_ids = row_start + jnp.arange(rows, dtype=jnp.int32)
    col_ids = col_start + jnp.arange(width, dtype=jnp.int32)

    own_map = lax.dynamic_index_in_dim(row_maps, side, 0, keepdims=False)
    other_map = lax.dynamic_index_in_dim(row_maps, 1 - side, 0, keepdims=False)
    first = front_pos * 2 * half + side * half
    own_rows = lax.dynamic_slice_in_dim(own_map, first, half) - row_start
    other_rows = lax.dynamic_slice_in_dim(other_map, first, half) - row_start
    blk_starts = col_start + blk * jnp.arange(nb, dtype=jnp.int32)[:, None]
    pair = 2 * grp
    parity = (col * nb * blk) // (lax.axis_size("front") * blk)
    own_cols = column_span(own_map, col, nb, grp).reshape(nb, pair) - blk_starts
    other_cols = column_span(other_map, col, nb, grp).reshape(nb, pair)
    other_cols = lax.dynamic_slice_in_dim(other_cols, parity * grp, grp, 1) - blk_starts

    local_block = child_blocks[0]
    kept_rows = lax.dynamic_slice_in_dim(local_block, side * half, half, 0)
    sent_rows = lax.dynamic_slice_in_dim(local_block, (1 - side) * half, half, 0)
    kept = column_span(kept_rows, col, nb, grp)
    sent_span = column_span(sent_rows, col, nb, grp)
    pick = one_hot(parity * grp + jnp.arange(grp, dtype=jnp.int32), pair, sent_span.dtype).T
    sent = jnp.concatenate(
        [
            jnp.dot(sent_span[:, j * pair : (j + 1) * pair], pick, preferred_element_type=jnp.float32)
            for j in range(nb)
        ],
        axis=1,
    ).astype(sent_span.dtype)
    arrived = swapped(sent, "cube", 0)
    own_part = place(kept, own_rows, own_cols, rows, blk)
    other_part = place(arrived, other_rows, other_cols, rows, blk)
    first_child = jnp.where(side == 0, own_part, other_part)
    second_child = jnp.where(side == 0, other_part, own_part)
    matrix = parent_front + first_child
    matrix = matrix + second_child

    live_rows = row_ids < front_size[0]
    live_cols = col_ids < front_size[0]
    matrix = jnp.where(live_rows[:, None] & live_cols[None, :], matrix, 0.0)
    matrix = matrix + jnp.where(
        (row_ids[:, None] == col_ids[None, :]) & jnp.logical_not(live_rows)[:, None], 1.0, 0.0
    )

    pcols = NP * PW
    head_local = matrix[:, :pcols]
    ncol = lax.axis_size("col")

    everyone = ("cube", "front", "col")
    ndev = lax.axis_size(everyone)
    nd = pcols // rows
    chunk = rows * pcols // ndev
    send = jnp.concatenate(
        [
            jnp.where((row_block == b) & (col == 0), head_local, 0.0).reshape(ndev, chunk)
            for b in range(nd)
        ],
        axis=1,
    )
    scattered = lax.all_to_all(send, everyone, 0, 0, tiled=True)
    src_index = [b * ncol for b in range(nd)]
    piece = jnp.concatenate(
        [scattered[src_index[b], b * chunk : (b + 1) * chunk] for b in range(nd)]
    )
    spread_out = jnp.broadcast_to(piece[None], (ndev, nd * chunk))
    gathered_top = lax.all_to_all(spread_out, everyone, 0, 0, tiled=True)
    top = jnp.concatenate(
        [gathered_top[:, b * chunk : (b + 1) * chunk].reshape(rows, pcols) for b in range(nd)],
        axis=0,
    )
    head_late, top = lax.optimization_barrier((head_local, top))
    arrived_heads = [lax.ppermute(head_late, "col", [(0, d)]) for d in range(1, ncol)]
    own = head_late
    for d, arrived_head in enumerate(arrived_heads, start=1):
        own = jnp.where(col == d, arrived_head, own)
    col_head = lax.dynamic_slice_in_dim(
        lax.all_gather(own, ("cube", "front"), tiled=True), col_start, width, 0
    )

    top_ids = jnp.arange(pcols, dtype=jnp.int32)
    eye = jnp.eye(PW, dtype=jnp.float32)
    inverses = []
    top_panels = []
    for index in range(NP):
        lower = index * PW
        diag_factor = jnp.linalg.cholesky(top[lower : lower + PW, lower : lower + PW])
        inverse = lax.linalg.triangular_solve(
            diag_factor, eye, left_side=True, lower=True, transpose_a=False
        )
        top_panel = jnp.dot(top[:, lower : lower + PW], inverse.T, precision=HI)
        top_panel = jnp.where((top_ids >= lower)[:, None], top_panel, 0.0)
        if index + 1 < NP:
            top = top - jnp.dot(top_panel, top_panel.T, precision=HI)
        inverses.append(inverse)
        top_panels.append(top_panel)

    panels = []
    for index in range(NP):
        lower = index * PW
        panel = jnp.dot(own[:, lower : lower + PW], inverses[index].T, precision=HI)
        panel = jnp.where((row_ids >= lower)[:, None], panel, 0.0)
        if index + 1 < NP:
            own = own - jnp.dot(panel, top_panels[index].T, precision=HI)
        panels.append(panel)
    factor = jnp.concatenate(panels, axis=1)

    blocks = {}
    for p in range(NP):
        blocks[p, p] = inverses[p]
        for i in range(p):
            acc = None
            for m in range(i, p):
                link = top_panels[m][p * PW : (p + 1) * PW]
                term = jnp.dot(link, blocks[m, i], precision=HI)
                acc = term if acc is None else acc + term
            blocks[p, i] = -jnp.dot(inverses[p], acc, precision=HI)
    zero = jnp.zeros((PW, PW), jnp.float32)
    top_inverse = jnp.concatenate(
        [jnp.concatenate([blocks.get((p, i), zero) for i in range(NP)], 1) for p in range(NP)], 0
    )
    weights = jnp.dot(factor, top_inverse, precision=HI)
    update = lax.dot_general(weights, col_head, (((1,), (1,)), ((), ())), precision=HI)
    matrix = matrix - update
    keep_rows = row_ids >= K
    keep_cols = col_ids >= K
    schur = jnp.where(keep_rows[:, None] & keep_cols[None, :], matrix, 0.0)
    return (factor, schur)


def solution(mesh):
    in_specs = (P(("cube", "front"), "col"), P("cube", "front", None), P(), P())
    out_specs = (P(("cube", "front"), None), P(("cube", "front"), "col"))
    return jax.shard_map(shards, mesh=mesh, in_specs=in_specs, out_specs=out_specs, check_vma=False)
```

```python
import jax
import jax.numpy as jnp
from jax import lax
from jax.sharding import PartitionSpec as P

PW = 256
NP = 2
K = 512

HI = lax.Precision.HIGHEST


def swapped(shard, axis, distance):
    return lax.ppermute(shard, axis, [(i, i ^ 1 << distance) for i in range(lax.axis_size(axis))])


def spread(block, axis, owner):
    block = jnp.where(lax.axis_index(axis) == owner, block, jnp.zeros_like(block))
    return lax.psum(block, axis)


def column_span(block, col, nb, grp):
    span = nb * 2 * grp
    start = (col * span) % block.shape[-1]
    return lax.dynamic_slice_in_dim(block, start, span, block.ndim - 1)


def one_hot(index, size, dtype):
    return (index[..., None] == jnp.arange(size, dtype=jnp.int32)).astype(dtype)


def place(part, row_local, col_local, rows, blk):
    nb, w = col_local.shape
    pr = one_hot(row_local, rows, part.dtype).T
    placed_rows = jnp.dot(pr, part, preferred_element_type=jnp.float32).astype(part.dtype)
    pieces = [
        jnp.dot(
            placed_rows[:, j * w : (j + 1) * w],
            one_hot(col_local[j], blk, part.dtype),
            preferred_element_type=jnp.float32,
        )
        for j in range(nb)
    ]
    return jnp.concatenate(pieces, axis=1)


def shards(parent_front, child_blocks, row_maps, front_size):
    rows, width = parent_front.shape
    half = child_blocks.shape[1] // 2
    grp = half
    blk = rows
    nb = width // blk
    side = lax.axis_index("cube")
    front_pos = lax.axis_index("front")
    col = lax.axis_index("col")
    row_block = lax.axis_index(("cube", "front"))
    row_start = row_block * rows
    col_start = col * width
    row_ids = row_start + jnp.arange(rows, dtype=jnp.int32)
    col_ids = col_start + jnp.arange(width, dtype=jnp.int32)

    own_map = lax.dynamic_index_in_dim(row_maps, side, 0, keepdims=False)
    other_map = lax.dynamic_index_in_dim(row_maps, 1 - side, 0, keepdims=False)
    first = front_pos * 2 * half + side * half
    own_rows = lax.dynamic_slice_in_dim(own_map, first, half) - row_start
    other_rows = lax.dynamic_slice_in_dim(other_map, first, half) - row_start
    blk_starts = col_start + blk * jnp.arange(nb, dtype=jnp.int32)[:, None]
    pair = 2 * grp
    parity = (col * nb * blk) // (lax.axis_size("front") * blk)
    own_cols = column_span(own_map, col, nb, grp).reshape(nb, pair) - blk_starts
    other_cols = column_span(other_map, col, nb, grp).reshape(nb, pair)
    other_cols = lax.dynamic_slice_in_dim(other_cols, parity * grp, grp, 1) - blk_starts

    local_block = child_blocks[0]
    kept_rows = lax.dynamic_slice_in_dim(local_block, side * half, half, 0)
    sent_rows = lax.dynamic_slice_in_dim(local_block, (1 - side) * half, half, 0)
    kept = column_span(kept_rows, col, nb, grp)
    sent_span = column_span(sent_rows, col, nb, grp)
    pick = one_hot(parity * grp + jnp.arange(grp, dtype=jnp.int32), pair, sent_span.dtype).T
    sent = jnp.concatenate(
        [
            jnp.dot(sent_span[:, j * pair : (j + 1) * pair], pick, preferred_element_type=jnp.float32)
            for j in range(nb)
        ],
        axis=1,
    ).astype(sent_span.dtype)
    arrived = swapped(sent, "cube", 0)
    own_part = place(kept, own_rows, own_cols, rows, blk)
    other_part = place(arrived, other_rows, other_cols, rows, blk)
    first_child = jnp.where(side == 0, own_part, other_part)
    second_child = jnp.where(side == 0, other_part, own_part)
    matrix = parent_front + first_child
    matrix = matrix + second_child

    live_rows = row_ids < front_size[0]
    live_cols = col_ids < front_size[0]
    matrix = jnp.where(live_rows[:, None] & live_cols[None, :], matrix, 0.0)
    matrix = matrix + jnp.where(
        (row_ids[:, None] == col_ids[None, :]) & jnp.logical_not(live_rows)[:, None], 1.0, 0.0
    )

    pcols = NP * PW
    head_local = matrix[:, :pcols]
    ncol = lax.axis_size("col")

    everyone = ("cube", "front", "col")
    ndev = lax.axis_size(everyone)
    nd = pcols // rows
    widths = [(b + 1) * PW for b in range(nd)]
    chunks = [rows * w // ndev for w in widths]
    send = jnp.concatenate(
        [
            jnp.where((row_block == b) & (col == 0), head_local[:, : widths[b]], 0.0).reshape(
                ndev, chunks[b]
            )
            for b in range(nd)
        ],
        axis=1,
    )
    scattered = lax.all_to_all(send, everyone, 0, 0, tiled=True)
    offsets = [sum(chunks[:b]) for b in range(nd)]
    piece = jnp.concatenate(
        [scattered[b * ncol, offsets[b] : offsets[b] + chunks[b]] for b in range(nd)]
    )
    spread_out = jnp.broadcast_to(piece[None], (ndev, sum(chunks)))
    gathered_top = lax.all_to_all(spread_out, everyone, 0, 0, tiled=True)
    lower_rows = [
        gathered_top[:, offsets[b] : offsets[b] + chunks[b]].reshape(rows, widths[b])
        for b in range(nd)
    ]
    top = jnp.concatenate(
        [
            jnp.concatenate(
                [lower_rows[b]] + [lower_rows[m][:, b * PW : (b + 1) * PW].T for m in range(b + 1, nd)],
                axis=1,
            )
            for b in range(nd)
        ],
        axis=0,
    )
    head_late, top = lax.optimization_barrier((head_local, top))
    arrived_heads = [lax.ppermute(head_late, "col", [(0, d)]) for d in range(1, ncol)]
    own = head_late
    for d, arrived_head in enumerate(arrived_heads, start=1):
        own = jnp.where(col == d, arrived_head, own)

    top_ids = jnp.arange(pcols, dtype=jnp.int32)
    eye = jnp.eye(PW, dtype=jnp.float32)
    inverses = []
    top_panels = []
    for index in range(NP):
        lower = index * PW
        diag_factor = jnp.linalg.cholesky(top[lower : lower + PW, lower : lower + PW])
        inverse = lax.linalg.triangular_solve(
            diag_factor, eye, left_side=True, lower=True, transpose_a=False
        )
        top_panel = jnp.dot(top[:, lower : lower + PW], inverse.T, precision=HI)
        top_panel = jnp.where((top_ids >= lower)[:, None], top_panel, 0.0)
        if index + 1 < NP:
            top = top - jnp.dot(top_panel, top_panel.T, precision=HI)
        inverses.append(inverse)
        top_panels.append(top_panel)
        if index == 0:
            own, inverse = lax.optimization_barrier((own, inverse))
            inverses[0] = inverse
            col_head = lax.dynamic_slice_in_dim(
                lax.all_gather(own, ("cube", "front"), tiled=True), col_start, width, 0
            )

    panels = []
    for index in range(NP):
        lower = index * PW
        panel = jnp.dot(own[:, lower : lower + PW], inverses[index].T, precision=HI)
        panel = jnp.where((row_ids >= lower)[:, None], panel, 0.0)
        if index + 1 < NP:
            own = own - jnp.dot(panel, top_panels[index].T, precision=HI)
        panels.append(panel)
    factor = jnp.concatenate(panels, axis=1)

    blocks = {}
    for p in range(NP):
        blocks[p, p] = inverses[p]
        for i in range(p):
            acc = None
            for m in range(i, p):
                link = top_panels[m][p * PW : (p + 1) * PW]
                term = jnp.dot(link, blocks[m, i], precision=HI)
                acc = term if acc is None else acc + term
            blocks[p, i] = -jnp.dot(inverses[p], acc, precision=HI)
    zero = jnp.zeros((PW, PW), jnp.float32)
    top_inverse = jnp.concatenate(
        [jnp.concatenate([blocks.get((p, i), zero) for i in range(NP)], 1) for p in range(NP)], 0
    )
    weights = jnp.dot(factor, top_inverse, precision=HI)
    update = lax.dot_general(weights, col_head, (((1,), (1,)), ((), ())), precision=HI)
    matrix = matrix - update
    keep_rows = row_ids >= K
    keep_cols = col_ids >= K
    schur = jnp.where(keep_rows[:, None] & keep_cols[None, :], matrix, 0.0)
    return (factor, schur)


def solution(mesh):
    in_specs = (P(("cube", "front"), "col"), P("cube", "front", None), P(), P())
    out_specs = (P(("cube", "front"), None), P(("cube", "front"), "col"))
    return jax.shard_map(shards, mesh=mesh, in_specs=in_specs, out_specs=out_specs, check_vma=False)
```

```python
import jax
import jax.numpy as jnp
from jax import lax
from jax.sharding import PartitionSpec as P

PW = 256
NP = 2
K = 512

HI = lax.Precision.HIGHEST


def swapped(shard, axis, distance):
    return lax.ppermute(shard, axis, [(i, i ^ 1 << distance) for i in range(lax.axis_size(axis))])


def spread(block, axis, owner):
    block = jnp.where(lax.axis_index(axis) == owner, block, jnp.zeros_like(block))
    return lax.psum(block, axis)


def column_span(block, col, nb, grp):
    span = nb * 2 * grp
    start = (col * span) % block.shape[-1]
    return lax.dynamic_slice_in_dim(block, start, span, block.ndim - 1)


def one_hot(index, size, dtype):
    return (index[..., None] == jnp.arange(size, dtype=jnp.int32)).astype(dtype)


def place(part, row_local, col_local, rows, blk):
    nb, w = col_local.shape
    pr = one_hot(row_local, rows, part.dtype).T
    placed_rows = jnp.dot(pr, part, preferred_element_type=jnp.float32).astype(part.dtype)
    pieces = [
        jnp.dot(
            placed_rows[:, j * w : (j + 1) * w],
            one_hot(col_local[j], blk, part.dtype),
            preferred_element_type=jnp.float32,
        )
        for j in range(nb)
    ]
    return jnp.concatenate(pieces, axis=1)


def shards(parent_front, child_blocks, row_maps, front_size):
    rows, width = parent_front.shape
    half = child_blocks.shape[1] // 2
    grp = half
    blk = rows
    nb = width // blk
    side = lax.axis_index("cube")
    front_pos = lax.axis_index("front")
    col = lax.axis_index("col")
    row_block = lax.axis_index(("cube", "front"))
    row_start = row_block * rows
    col_start = col * width
    row_ids = row_start + jnp.arange(rows, dtype=jnp.int32)
    col_ids = col_start + jnp.arange(width, dtype=jnp.int32)

    own_map = lax.dynamic_index_in_dim(row_maps, side, 0, keepdims=False)
    other_map = lax.dynamic_index_in_dim(row_maps, 1 - side, 0, keepdims=False)
    first = front_pos * 2 * half + side * half
    own_rows = lax.dynamic_slice_in_dim(own_map, first, half) - row_start
    other_rows = lax.dynamic_slice_in_dim(other_map, first, half) - row_start
    blk_starts = col_start + blk * jnp.arange(nb, dtype=jnp.int32)[:, None]
    pair = 2 * grp
    parity = (col * nb * blk) // (lax.axis_size("front") * blk)
    own_cols = column_span(own_map, col, nb, grp).reshape(nb, pair) - blk_starts
    other_cols = column_span(other_map, col, nb, grp).reshape(nb, pair)
    other_cols = lax.dynamic_slice_in_dim(other_cols, parity * grp, grp, 1) - blk_starts

    local_block = child_blocks[0]
    kept_rows = lax.dynamic_slice_in_dim(local_block, side * half, half, 0)
    sent_rows = lax.dynamic_slice_in_dim(local_block, (1 - side) * half, half, 0)
    kept = column_span(kept_rows, col, nb, grp)
    sent_span = column_span(sent_rows, col, nb, grp)
    pick = one_hot(parity * grp + jnp.arange(grp, dtype=jnp.int32), pair, sent_span.dtype).T
    sent = jnp.concatenate(
        [
            jnp.dot(sent_span[:, j * pair : (j + 1) * pair], pick, preferred_element_type=jnp.float32)
            for j in range(nb)
        ],
        axis=1,
    ).astype(sent_span.dtype)
    arrived = swapped(sent, "cube", 0)
    own_part = place(kept, own_rows, own_cols, rows, blk)
    other_part = place(arrived, other_rows, other_cols, rows, blk)
    first_child = jnp.where(side == 0, own_part, other_part)
    second_child = jnp.where(side == 0, other_part, own_part)
    matrix = parent_front + first_child
    matrix = matrix + second_child

    live_rows = row_ids < front_size[0]
    live_cols = col_ids < front_size[0]
    matrix = jnp.where(live_rows[:, None] & live_cols[None, :], matrix, 0.0)
    matrix = matrix + jnp.where(
        (row_ids[:, None] == col_ids[None, :]) & jnp.logical_not(live_rows)[:, None], 1.0, 0.0
    )

    pcols = NP * PW
    head_local = matrix[:, :pcols]
    ncol = lax.axis_size("col")

    everyone = ("cube", "front", "col")
    ndev = lax.axis_size(everyone)
    nd = pcols // rows
    widths = [(b + 1) * PW for b in range(nd)]
    chunks = [rows * w // ndev for w in widths]
    send = jnp.concatenate(
        [
            jnp.where((row_block == b) & (col == 0), head_local[:, : widths[b]], 0.0).reshape(
                ndev, chunks[b]
            )
            for b in range(nd)
        ],
        axis=1,
    )
    scattered = lax.all_to_all(send, everyone, 0, 0, tiled=True)
    offsets = [sum(chunks[:b]) for b in range(nd)]
    piece = jnp.concatenate(
        [scattered[b * ncol, offsets[b] : offsets[b] + chunks[b]] for b in range(nd)]
    )
    spread_out = jnp.broadcast_to(piece[None], (ndev, sum(chunks)))
    gathered_top = lax.all_to_all(spread_out, everyone, 0, 0, tiled=True)
    lower_rows = [
        gathered_top[:, offsets[b] : offsets[b] + chunks[b]].reshape(rows, widths[b])
        for b in range(nd)
    ]
    top = jnp.concatenate(
        [
            jnp.concatenate(
                [lower_rows[b]] + [lower_rows[m][:, b * PW : (b + 1) * PW].T for m in range(b + 1, nd)],
                axis=1,
            )
            for b in range(nd)
        ],
        axis=0,
    )
    head_late, top = lax.optimization_barrier((head_local, top))
    arrived_heads = [lax.ppermute(head_late, "col", [(0, d)]) for d in range(1, ncol)]
    own = head_late
    for d, arrived_head in enumerate(arrived_heads, start=1):
        own = jnp.where(col == d, arrived_head, own)

    bw = PW // 2 if PW % 256 == 0 else PW
    nblk = pcols // bw
    eye = jnp.eye(bw, dtype=jnp.float32)
    trail = top
    diag_inverse = []
    low = {}
    for j in range(nblk):
        diag_factor = jnp.linalg.cholesky(trail[:bw, :bw])
        inverse = lax.linalg.triangular_solve(
            diag_factor, eye, left_side=True, lower=True, transpose_a=False
        )
        diag_inverse.append(inverse)
        if j == 0:
            own, inverse = lax.optimization_barrier((own, inverse))
            diag_inverse[0] = inverse
            col_head = lax.dynamic_slice_in_dim(
                lax.all_gather(own, ("cube", "front"), tiled=True), col_start, width, 0
            )
        if j + 1 < nblk:
            below = jnp.dot(trail[bw:, :bw], inverse.T, precision=HI)
            for i in range(j + 1, nblk):
                low[i, j] = below[(i - j - 1) * bw : (i - j) * bw]
            trail = trail[bw:, bw:] - jnp.dot(below, below.T, precision=HI)

    top_inverse = diag_inverse[0]
    for p in range(1, nblk):
        links = jnp.concatenate([low[p, m] for m in range(p)], axis=1)
        left = -jnp.dot(diag_inverse[p], jnp.dot(links, top_inverse, precision=HI), precision=HI)
        top_inverse = jnp.concatenate(
            [
                jnp.concatenate([top_inverse, jnp.zeros((p * bw, bw), jnp.float32)], axis=1),
                jnp.concatenate([left, diag_inverse[p]], axis=1),
            ],
            axis=0,
        )

    factor = jnp.dot(own, top_inverse.T, precision=HI)
    factor_cols = jnp.arange(pcols, dtype=jnp.int32)
    factor = jnp.where(row_ids[:, None] >= (factor_cols // PW * PW)[None, :], factor, 0.0)
    weights = jnp.dot(factor, top_inverse, precision=HI)
    update = lax.dot_general(weights, col_head, (((1,), (1,)), ((), ())), precision=HI)
    matrix = matrix - update
    keep_rows = row_ids >= K
    keep_cols = col_ids >= K
    schur = jnp.where(keep_rows[:, None] & keep_cols[None, :], matrix, 0.0)
    return (factor, schur)


def solution(mesh):
    in_specs = (P(("cube", "front"), "col"), P("cube", "front", None), P(), P())
    out_specs = (P(("cube", "front"), None), P(("cube", "front"), "col"))
    return jax.shard_map(shards, mesh=mesh, in_specs=in_specs, out_specs=out_specs, check_vma=False)
```

```python
import jax
import jax.numpy as jnp
from jax import lax
from jax.sharding import PartitionSpec as P

PW = 256
NP = 2
K = 512

HI = lax.Precision.HIGHEST


def swapped(shard, axis, distance):
    return lax.ppermute(shard, axis, [(i, i ^ 1 << distance) for i in range(lax.axis_size(axis))])


def spread(block, axis, owner):
    block = jnp.where(lax.axis_index(axis) == owner, block, jnp.zeros_like(block))
    return lax.psum(block, axis)


def column_span(block, col, nb, grp):
    span = nb * 2 * grp
    start = (col * span) % block.shape[-1]
    return lax.dynamic_slice_in_dim(block, start, span, block.ndim - 1)


def one_hot(index, size, dtype):
    return (index[..., None] == jnp.arange(size, dtype=jnp.int32)).astype(dtype)


def place(part, row_local, col_local, rows, blk):
    nb, w = col_local.shape
    pr = one_hot(row_local, rows, part.dtype).T
    placed_rows = jnp.dot(pr, part, preferred_element_type=jnp.float32).astype(part.dtype)
    pieces = [
        jnp.dot(
            placed_rows[:, j * w : (j + 1) * w],
            one_hot(col_local[j], blk, part.dtype),
            preferred_element_type=jnp.float32,
        )
        for j in range(nb)
    ]
    return jnp.concatenate(pieces, axis=1)


def shards(parent_front, child_blocks, row_maps, front_size):
    rows, width = parent_front.shape
    half = child_blocks.shape[1] // 2
    grp = half
    blk = rows
    nb = width // blk
    side = lax.axis_index("cube")
    front_pos = lax.axis_index("front")
    col = lax.axis_index("col")
    row_block = lax.axis_index(("cube", "front"))
    row_start = row_block * rows
    col_start = col * width
    row_ids = row_start + jnp.arange(rows, dtype=jnp.int32)
    col_ids = col_start + jnp.arange(width, dtype=jnp.int32)

    own_map = lax.dynamic_index_in_dim(row_maps, side, 0, keepdims=False)
    other_map = lax.dynamic_index_in_dim(row_maps, 1 - side, 0, keepdims=False)
    first = front_pos * 2 * half + side * half
    own_rows = lax.dynamic_slice_in_dim(own_map, first, half) - row_start
    other_rows = lax.dynamic_slice_in_dim(other_map, first, half) - row_start
    blk_starts = col_start + blk * jnp.arange(nb, dtype=jnp.int32)[:, None]
    pair = 2 * grp
    parity = (col * nb * blk) // (lax.axis_size("front") * blk)
    own_cols = column_span(own_map, col, nb, grp).reshape(nb, pair) - blk_starts
    other_cols = column_span(other_map, col, nb, grp).reshape(nb, pair)
    other_cols = lax.dynamic_slice_in_dim(other_cols, parity * grp, grp, 1) - blk_starts

    local_block = child_blocks[0]
    kept_rows = lax.dynamic_slice_in_dim(local_block, side * half, half, 0)
    sent_rows = lax.dynamic_slice_in_dim(local_block, (1 - side) * half, half, 0)
    kept = column_span(kept_rows, col, nb, grp)
    sent_span = column_span(sent_rows, col, nb, grp)
    pick = one_hot(parity * grp + jnp.arange(grp, dtype=jnp.int32), pair, sent_span.dtype).T
    sent = jnp.concatenate(
        [
            jnp.dot(sent_span[:, j * pair : (j + 1) * pair], pick, preferred_element_type=jnp.float32)
            for j in range(nb)
        ],
        axis=1,
    ).astype(sent_span.dtype)
    arrived = swapped(sent, "cube", 0)
    own_part = place(kept, own_rows, own_cols, rows, blk)
    other_part = place(arrived, other_rows, other_cols, rows, blk)
    first_child = jnp.where(side == 0, own_part, other_part)
    second_child = jnp.where(side == 0, other_part, own_part)
    matrix = parent_front + first_child
    matrix = matrix + second_child

    live_rows = row_ids < front_size[0]
    live_cols = col_ids < front_size[0]
    matrix = jnp.where(live_rows[:, None] & live_cols[None, :], matrix, 0.0)
    matrix = matrix + jnp.where(
        (row_ids[:, None] == col_ids[None, :]) & jnp.logical_not(live_rows)[:, None], 1.0, 0.0
    )

    pcols = NP * PW
    head_local = matrix[:, :pcols]
    ncol = lax.axis_size("col")

    everyone = ("cube", "front", "col")
    ndev = lax.axis_size(everyone)
    nd = pcols // rows
    widths = [(b + 1) * PW for b in range(nd)]
    chunks = [rows * w // ndev for w in widths]
    send = jnp.concatenate(
        [
            jnp.where((row_block == b) & (col == 0), head_local[:, : widths[b]], 0.0).reshape(
                ndev, chunks[b]
            )
            for b in range(nd)
        ],
        axis=1,
    )
    scattered = lax.all_to_all(send, everyone, 0, 0, tiled=True)
    offsets = [sum(chunks[:b]) for b in range(nd)]
    piece = jnp.concatenate(
        [scattered[b * ncol, offsets[b] : offsets[b] + chunks[b]] for b in range(nd)]
    )
    spread_out = jnp.broadcast_to(piece[None], (ndev, sum(chunks)))
    gathered_top = lax.all_to_all(spread_out, everyone, 0, 0, tiled=True)
    lower_rows = [
        gathered_top[:, offsets[b] : offsets[b] + chunks[b]].reshape(rows, widths[b])
        for b in range(nd)
    ]
    top = jnp.concatenate(
        [
            jnp.concatenate(
                [lower_rows[b]] + [lower_rows[m][:, b * PW : (b + 1) * PW].T for m in range(b + 1, nd)],
                axis=1,
            )
            for b in range(nd)
        ],
        axis=0,
    )
    head_late, top = lax.optimization_barrier((head_local, top))
    arrived_heads = [lax.ppermute(head_late, "col", [(0, d)]) for d in range(1, ncol)]
    own = head_late
    for d, arrived_head in enumerate(arrived_heads, start=1):
        own = jnp.where(col == d, arrived_head, own)

    bw = PW // 4 if PW % 256 == 0 else PW
    nblk = pcols // bw
    eye = jnp.eye(bw, dtype=jnp.float32)
    trail = top
    diag_inverse = []
    low = {}
    for j in range(nblk):
        diag_factor = jnp.linalg.cholesky(trail[:bw, :bw])
        inverse = lax.linalg.triangular_solve(
            diag_factor, eye, left_side=True, lower=True, transpose_a=False
        )
        diag_inverse.append(inverse)
        if j == 0:
            own, inverse = lax.optimization_barrier((own, inverse))
            diag_inverse[0] = inverse
            col_head = lax.dynamic_slice_in_dim(
                lax.all_gather(own, ("cube", "front"), tiled=True), col_start, width, 0
            )
        if j + 1 < nblk:
            below = jnp.dot(trail[bw:, :bw], inverse.T, precision=HI)
            for i in range(j + 1, nblk):
                low[i, j] = below[(i - j - 1) * bw : (i - j) * bw]
            trail = trail[bw:, bw:] - jnp.dot(below, below.T, precision=HI)

    top_inverse = diag_inverse[0]
    for p in range(1, nblk):
        links = jnp.concatenate([low[p, m] for m in range(p)], axis=1)
        left = -jnp.dot(diag_inverse[p], jnp.dot(links, top_inverse, precision=HI), precision=HI)
        top_inverse = jnp.concatenate(
            [
                jnp.concatenate([top_inverse, jnp.zeros((p * bw, bw), jnp.float32)], axis=1),
                jnp.concatenate([left, diag_inverse[p]], axis=1),
            ],
            axis=0,
        )

    factor = jnp.dot(own, top_inverse.T, precision=HI)
    factor_cols = jnp.arange(pcols, dtype=jnp.int32)
    factor = jnp.where(row_ids[:, None] >= (factor_cols // PW * PW)[None, :], factor, 0.0)
    weights = jnp.dot(factor, top_inverse, precision=HI)
    update = lax.dot_general(weights, col_head, (((1,), (1,)), ((), ())), precision=HI)
    matrix = matrix - update
    keep_rows = row_ids >= K
    keep_cols = col_ids >= K
    schur = jnp.where(keep_rows[:, None] & keep_cols[None, :], matrix, 0.0)
    return (factor, schur)


def solution(mesh):
    in_specs = (P(("cube", "front"), "col"), P("cube", "front", None), P(), P())
    out_specs = (P(("cube", "front"), None), P(("cube", "front"), "col"))
    return jax.shard_map(shards, mesh=mesh, in_specs=in_specs, out_specs=out_specs, check_vma=False)
```

```python
import jax
import jax.numpy as jnp
from jax import lax
from jax.sharding import PartitionSpec as P

PW = 256
NP = 2
K = 512

HI = lax.Precision.HIGHEST


def swapped(shard, axis, distance):
    return lax.ppermute(shard, axis, [(i, i ^ 1 << distance) for i in range(lax.axis_size(axis))])


def spread(block, axis, owner):
    block = jnp.where(lax.axis_index(axis) == owner, block, jnp.zeros_like(block))
    return lax.psum(block, axis)


def column_span(block, col, nb, grp):
    span = nb * 2 * grp
    start = (col * span) % block.shape[-1]
    return lax.dynamic_slice_in_dim(block, start, span, block.ndim - 1)


def one_hot(index, size, dtype):
    return (index[..., None] == jnp.arange(size, dtype=jnp.int32)).astype(dtype)


def place(part, row_local, col_local, rows, blk):
    nb, w = col_local.shape
    pr = one_hot(row_local, rows, part.dtype).T
    placed_rows = jnp.dot(pr, part, preferred_element_type=jnp.float32).astype(part.dtype)
    pieces = [
        jnp.dot(
            placed_rows[:, j * w : (j + 1) * w],
            one_hot(col_local[j], blk, part.dtype),
            preferred_element_type=jnp.float32,
        )
        for j in range(nb)
    ]
    return jnp.concatenate(pieces, axis=1)


def shards(parent_front, child_blocks, row_maps, front_size):
    rows, width = parent_front.shape
    half = child_blocks.shape[1] // 2
    grp = half
    blk = rows
    nb = width // blk
    side = lax.axis_index("cube")
    front_pos = lax.axis_index("front")
    col = lax.axis_index("col")
    row_block = lax.axis_index(("cube", "front"))
    row_start = row_block * rows
    col_start = col * width
    row_ids = row_start + jnp.arange(rows, dtype=jnp.int32)
    col_ids = col_start + jnp.arange(width, dtype=jnp.int32)

    own_map = lax.dynamic_index_in_dim(row_maps, side, 0, keepdims=False)
    other_map = lax.dynamic_index_in_dim(row_maps, 1 - side, 0, keepdims=False)
    first = front_pos * 2 * half + side * half
    own_rows = lax.dynamic_slice_in_dim(own_map, first, half) - row_start
    other_rows = lax.dynamic_slice_in_dim(other_map, first, half) - row_start
    blk_starts = col_start + blk * jnp.arange(nb, dtype=jnp.int32)[:, None]
    pair = 2 * grp
    parity = (col * nb * blk) // (lax.axis_size("front") * blk)
    own_cols = column_span(own_map, col, nb, grp).reshape(nb, pair) - blk_starts
    other_cols = column_span(other_map, col, nb, grp).reshape(nb, pair)
    other_cols = lax.dynamic_slice_in_dim(other_cols, parity * grp, grp, 1) - blk_starts

    local_block = child_blocks[0]
    kept_rows = lax.dynamic_slice_in_dim(local_block, side * half, half, 0)
    sent_rows = lax.dynamic_slice_in_dim(local_block, (1 - side) * half, half, 0)
    kept = column_span(kept_rows, col, nb, grp)
    sent_span = column_span(sent_rows, col, nb, grp)
    pick = one_hot(parity * grp + jnp.arange(grp, dtype=jnp.int32), pair, sent_span.dtype).T
    sent = jnp.concatenate(
        [
            jnp.dot(sent_span[:, j * pair : (j + 1) * pair], pick, preferred_element_type=jnp.float32)
            for j in range(nb)
        ],
        axis=1,
    ).astype(sent_span.dtype)
    pcols = NP * PW
    hb = pcols // blk
    arrived_head = swapped(sent[:, : hb * grp], "cube", 0)
    arrived_rest = swapped(sent[:, hb * grp :], "cube", 0)
    arrived = jnp.concatenate([arrived_head, arrived_rest], axis=1)

    def assemble(nblocks, arrived_part):
        span = nblocks * blk
        own_part = place(kept[:, : nblocks * pair], own_rows, own_cols[:nblocks], rows, blk)
        other_part = place(arrived_part, other_rows, other_cols[:nblocks], rows, blk)
        first_child = jnp.where(side == 0, own_part, other_part)
        second_child = jnp.where(side == 0, other_part, own_part)
        part = parent_front[:, :span] + first_child
        part = part + second_child
        ids = col_ids[:span]
        live_rows = row_ids < front_size[0]
        live_cols = ids < front_size[0]
        part = jnp.where(live_rows[:, None] & live_cols[None, :], part, 0.0)
        return part + jnp.where(
            (row_ids[:, None] == ids[None, :]) & jnp.logical_not(live_rows)[:, None], 1.0, 0.0
        )

    head_local = assemble(hb, arrived_head)
    matrix = assemble(nb, arrived)

    ncol = lax.axis_size("col")

    everyone = ("cube", "front", "col")
    ndev = lax.axis_size(everyone)
    nd = pcols // rows
    widths = [(b + 1) * PW for b in range(nd)]
    chunks = [rows * w // ndev for w in widths]
    send = jnp.concatenate(
        [
            jnp.where((row_block == b) & (col == 0), head_local[:, : widths[b]], 0.0).reshape(
                ndev, chunks[b]
            )
            for b in range(nd)
        ],
        axis=1,
    )
    scattered = lax.all_to_all(send, everyone, 0, 0, tiled=True)
    offsets = [sum(chunks[:b]) for b in range(nd)]
    piece = jnp.concatenate(
        [scattered[b * ncol, offsets[b] : offsets[b] + chunks[b]] for b in range(nd)]
    )
    spread_out = jnp.broadcast_to(piece[None], (ndev, sum(chunks)))
    gathered_top = lax.all_to_all(spread_out, everyone, 0, 0, tiled=True)
    lower_rows = [
        gathered_top[:, offsets[b] : offsets[b] + chunks[b]].reshape(rows, widths[b])
        for b in range(nd)
    ]
    top = jnp.concatenate(
        [
            jnp.concatenate(
                [lower_rows[b]] + [lower_rows[m][:, b * PW : (b + 1) * PW].T for m in range(b + 1, nd)],
                axis=1,
            )
            for b in range(nd)
        ],
        axis=0,
    )
    head_late, top = lax.optimization_barrier((head_local, top))
    arrived_heads = [lax.ppermute(head_late, "col", [(0, d)]) for d in range(1, ncol)]
    own = head_late
    for d, arrived_head in enumerate(arrived_heads, start=1):
        own = jnp.where(col == d, arrived_head, own)

    bw = PW // 2 if PW % 256 == 0 else PW
    nblk = pcols // bw
    eye = jnp.eye(bw, dtype=jnp.float32)
    trail = top
    diag_inverse = []
    low = {}
    for j in range(nblk):
        diag_factor = jnp.linalg.cholesky(trail[:bw, :bw])
        inverse = lax.linalg.triangular_solve(
            diag_factor, eye, left_side=True, lower=True, transpose_a=False
        )
        diag_inverse.append(inverse)
        if j == 0:
            own, inverse = lax.optimization_barrier((own, inverse))
            diag_inverse[0] = inverse
            col_head = lax.dynamic_slice_in_dim(
                lax.all_gather(own, ("cube", "front"), tiled=True), col_start, width, 0
            )
        if j + 1 < nblk:
            below = jnp.dot(trail[bw:, :bw], inverse.T, precision=HI)
            for i in range(j + 1, nblk):
                low[i, j] = below[(i - j - 1) * bw : (i - j) * bw]
            trail = trail[bw:, bw:] - jnp.dot(below, below.T, precision=HI)

    top_inverse = diag_inverse[0]
    for p in range(1, nblk):
        links = jnp.concatenate([low[p, m] for m in range(p)], axis=1)
        left = -jnp.dot(diag_inverse[p], jnp.dot(links, top_inverse, precision=HI), precision=HI)
        top_inverse = jnp.concatenate(
            [
                jnp.concatenate([top_inverse, jnp.zeros((p * bw, bw), jnp.float32)], axis=1),
                jnp.concatenate([left, diag_inverse[p]], axis=1),
            ],
            axis=0,
        )

    factor = jnp.dot(own, top_inverse.T, precision=HI)
    factor_cols = jnp.arange(pcols, dtype=jnp.int32)
    factor = jnp.where(row_ids[:, None] >= (factor_cols // PW * PW)[None, :], factor, 0.0)
    weights = jnp.dot(factor, top_inverse, precision=HI)
    update = lax.dot_general(
        weights, col_head, (((1,), (1,)), ((), ())), precision=lax.Precision.HIGH
    )
    matrix = matrix - update
    keep_rows = row_ids >= K
    keep_cols = col_ids >= K
    schur = jnp.where(keep_rows[:, None] & keep_cols[None, :], matrix, 0.0)
    return (factor, schur)


def solution(mesh):
    in_specs = (P(("cube", "front"), "col"), P("cube", "front", None), P(), P())
    out_specs = (P(("cube", "front"), None), P(("cube", "front"), "col"))
    return jax.shard_map(shards, mesh=mesh, in_specs=in_specs, out_specs=out_specs, check_vma=False)
```

```python
import jax
import jax.numpy as jnp
from jax import lax
from jax.sharding import PartitionSpec as P

PW = 256
NP = 2
K = 512

HI = lax.Precision.HIGHEST


def swapped(shard, axis, distance):
    return lax.ppermute(shard, axis, [(i, i ^ 1 << distance) for i in range(lax.axis_size(axis))])


def spread(block, axis, owner):
    block = jnp.where(lax.axis_index(axis) == owner, block, jnp.zeros_like(block))
    return lax.psum(block, axis)


def column_span(block, col, nb, grp):
    span = nb * 2 * grp
    start = (col * span) % block.shape[-1]
    return lax.dynamic_slice_in_dim(block, start, span, block.ndim - 1)


def one_hot(index, size, dtype):
    return (index[..., None] == jnp.arange(size, dtype=jnp.int32)).astype(dtype)


def place(part, row_local, col_local, rows, blk):
    nb, w = col_local.shape
    pr = one_hot(row_local, rows, part.dtype).T
    placed_rows = jnp.dot(pr, part, preferred_element_type=jnp.float32).astype(part.dtype)
    pieces = [
        jnp.dot(
            placed_rows[:, j * w : (j + 1) * w],
            one_hot(col_local[j], blk, part.dtype),
            preferred_element_type=jnp.float32,
        )
        for j in range(nb)
    ]
    return jnp.concatenate(pieces, axis=1)


def gather_column_rows(own, col):
    ncube, nfront, ncol = (lax.axis_size(a) for a in ("cube", "front", "col"))
    rows = own.shape[0]
    per_range = ncube * nfront // ncol
    pieces = nfront // per_range
    lin = lambda c, f, k: (c * nfront + f) * ncol + k
    pairs = []
    for c in range(ncube):
        for f in range(nfront):
            for k in range(ncol):
                block = per_range * k + f % per_range
                src = lin(block // nfront, block % nfront, pieces * c + f // per_range)
                pairs.append((src, lin(c, f, k)))
    part = rows // pieces
    me_piece = (col % pieces) * part
    moved = lax.ppermute(
        lax.dynamic_slice_in_dim(own, me_piece, part, 0), ("cube", "front", "col"), pairs
    )
    spread = jnp.broadcast_to(moved[None], (nfront,) + moved.shape)
    got = lax.all_to_all(spread, "front", 0, 0, tiled=True)
    got = got.reshape(pieces, per_range, part, own.shape[1]).transpose(1, 0, 2, 3)
    return got.reshape(per_range * rows, own.shape[1])


def shards(parent_front, child_blocks, row_maps, front_size):
    rows, width = parent_front.shape
    half = child_blocks.shape[1] // 2
    grp = half
    blk = rows
    nb = width // blk
    side = lax.axis_index("cube")
    front_pos = lax.axis_index("front")
    col = lax.axis_index("col")
    row_block = lax.axis_index(("cube", "front"))
    row_start = row_block * rows
    col_start = col * width
    row_ids = row_start + jnp.arange(rows, dtype=jnp.int32)
    col_ids = col_start + jnp.arange(width, dtype=jnp.int32)

    own_map = lax.dynamic_index_in_dim(row_maps, side, 0, keepdims=False)
    other_map = lax.dynamic_index_in_dim(row_maps, 1 - side, 0, keepdims=False)
    first = front_pos * 2 * half + side * half
    own_rows = lax.dynamic_slice_in_dim(own_map, first, half) - row_start
    other_rows = lax.dynamic_slice_in_dim(other_map, first, half) - row_start
    blk_starts = col_start + blk * jnp.arange(nb, dtype=jnp.int32)[:, None]
    pair = 2 * grp
    parity = (col * nb * blk) // (lax.axis_size("front") * blk)
    own_cols = column_span(own_map, col, nb, grp).reshape(nb, pair) - blk_starts
    other_cols = column_span(other_map, col, nb, grp).reshape(nb, pair)
    other_cols = lax.dynamic_slice_in_dim(other_cols, parity * grp, grp, 1) - blk_starts

    local_block = child_blocks[0]
    kept_rows = lax.dynamic_slice_in_dim(local_block, side * half, half, 0)
    sent_rows = lax.dynamic_slice_in_dim(local_block, (1 - side) * half, half, 0)
    kept = column_span(kept_rows, col, nb, grp)
    sent_span = column_span(sent_rows, col, nb, grp)
    pick = one_hot(parity * grp + jnp.arange(grp, dtype=jnp.int32), pair, sent_span.dtype).T
    sent = jnp.concatenate(
        [
            jnp.dot(sent_span[:, j * pair : (j + 1) * pair], pick, preferred_element_type=jnp.float32)
            for j in range(nb)
        ],
        axis=1,
    ).astype(sent_span.dtype)
    arrived = swapped(sent, "cube", 0)
    own_part = place(kept, own_rows, own_cols, rows, blk)
    other_part = place(arrived, other_rows, other_cols, rows, blk)
    first_child = jnp.where(side == 0, own_part, other_part)
    second_child = jnp.where(side == 0, other_part, own_part)
    matrix = parent_front + first_child
    matrix = matrix + second_child

    live_rows = row_ids < front_size[0]
    live_cols = col_ids < front_size[0]
    matrix = jnp.where(live_rows[:, None] & live_cols[None, :], matrix, 0.0)
    matrix = matrix + jnp.where(
        (row_ids[:, None] == col_ids[None, :]) & jnp.logical_not(live_rows)[:, None], 1.0, 0.0
    )

    pcols = NP * PW
    head_local = matrix[:, :pcols]
    ncol = lax.axis_size("col")

    everyone = ("cube", "front", "col")
    ndev = lax.axis_size(everyone)
    nd = pcols // rows
    widths = [(b + 1) * PW for b in range(nd)]
    chunks = [rows * w // ndev for w in widths]
    send = jnp.concatenate(
        [
            jnp.where((row_block == b) & (col == 0), head_local[:, : widths[b]], 0.0).reshape(
                ndev, chunks[b]
            )
            for b in range(nd)
        ],
        axis=1,
    )
    scattered = lax.all_to_all(send, everyone, 0, 0, tiled=True)
    offsets = [sum(chunks[:b]) for b in range(nd)]
    piece = jnp.concatenate(
        [scattered[b * ncol, offsets[b] : offsets[b] + chunks[b]] for b in range(nd)]
    )
    spread_out = jnp.broadcast_to(piece[None], (ndev, sum(chunks)))
    gathered_top = lax.all_to_all(spread_out, everyone, 0, 0, tiled=True)
    lower_rows = [
        gathered_top[:, offsets[b] : offsets[b] + chunks[b]].reshape(rows, widths[b])
        for b in range(nd)
    ]
    top = jnp.concatenate(
        [
            jnp.concatenate(
                [lower_rows[b]] + [lower_rows[m][:, b * PW : (b + 1) * PW].T for m in range(b + 1, nd)],
                axis=1,
            )
            for b in range(nd)
        ],
        axis=0,
    )
    head_late, top = lax.optimization_barrier((head_local, top))
    arrived_heads = [lax.ppermute(head_late, "col", [(0, d)]) for d in range(1, ncol)]
    own = head_late
    for d, arrived_head in enumerate(arrived_heads, start=1):
        own = jnp.where(col == d, arrived_head, own)

    bw = PW // 2 if PW % 256 == 0 else PW
    nblk = pcols // bw
    eye = jnp.eye(bw, dtype=jnp.float32)
    trail = top
    diag_inverse = []
    low = {}
    for j in range(nblk):
        diag_factor = jnp.linalg.cholesky(trail[:bw, :bw])
        inverse = lax.linalg.triangular_solve(
            diag_factor, eye, left_side=True, lower=True, transpose_a=False
        )
        diag_inverse.append(inverse)
        if j == 0:
            own, inverse = lax.optimization_barrier((own, inverse))
            diag_inverse[0] = inverse
            col_head = gather_column_rows(own, col)
        if j + 1 < nblk:
            below = jnp.dot(trail[bw:, :bw], inverse.T, precision=HI)
            for i in range(j + 1, nblk):
                low[i, j] = below[(i - j - 1) * bw : (i - j) * bw]
            trail = trail[bw:, bw:] - jnp.dot(below, below.T, precision=HI)

    top_inverse = diag_inverse[0]
    for p in range(1, nblk):
        links = jnp.concatenate([low[p, m] for m in range(p)], axis=1)
        left = -jnp.dot(diag_inverse[p], jnp.dot(links, top_inverse, precision=HI), precision=HI)
        top_inverse = jnp.concatenate(
            [
                jnp.concatenate([top_inverse, jnp.zeros((p * bw, bw), jnp.float32)], axis=1),
                jnp.concatenate([left, diag_inverse[p]], axis=1),
            ],
            axis=0,
        )

    factor = jnp.dot(own, top_inverse.T, precision=HI)
    factor_cols = jnp.arange(pcols, dtype=jnp.int32)
    factor = jnp.where(row_ids[:, None] >= (factor_cols // PW * PW)[None, :], factor, 0.0)
    weights = jnp.dot(factor, top_inverse, precision=HI)
    update = lax.dot_general(weights, col_head, (((1,), (1,)), ((), ())), precision=HI)
    matrix = matrix - update
    keep_rows = row_ids >= K
    keep_cols = col_ids >= K
    schur = jnp.where(keep_rows[:, None] & keep_cols[None, :], matrix, 0.0)
    return (factor, schur)


def solution(mesh):
    in_specs = (P(("cube", "front"), "col"), P("cube", "front", None), P(), P())
    out_specs = (P(("cube", "front"), None), P(("cube", "front"), "col"))
    return jax.shard_map(shards, mesh=mesh, in_specs=in_specs, out_specs=out_specs, check_vma=False)
```

```python
import jax
import jax.numpy as jnp
from jax import lax
from jax.sharding import PartitionSpec as P

PW = 256
NP = 2
K = 512

HI = lax.Precision.HIGHEST


def swapped(shard, axis, distance):
    return lax.ppermute(shard, axis, [(i, i ^ 1 << distance) for i in range(lax.axis_size(axis))])


def spread(block, axis, owner):
    block = jnp.where(lax.axis_index(axis) == owner, block, jnp.zeros_like(block))
    return lax.psum(block, axis)


def column_span(block, col, nb, grp):
    span = nb * 2 * grp
    start = (col * span) % block.shape[-1]
    return lax.dynamic_slice_in_dim(block, start, span, block.ndim - 1)


def one_hot(index, size, dtype):
    return (index[..., None] == jnp.arange(size, dtype=jnp.int32)).astype(dtype)


def place(part, row_local, col_local, rows, blk):
    nb, w = col_local.shape
    pr = one_hot(row_local, rows, part.dtype).T
    placed_rows = jnp.dot(pr, part, preferred_element_type=jnp.float32).astype(part.dtype)
    pieces = [
        jnp.dot(
            placed_rows[:, j * w : (j + 1) * w],
            one_hot(col_local[j], blk, part.dtype),
            preferred_element_type=jnp.float32,
        )
        for j in range(nb)
    ]
    return jnp.concatenate(pieces, axis=1)


def shards(parent_front, child_blocks, row_maps, front_size):
    rows, width = parent_front.shape
    half = child_blocks.shape[1] // 2
    grp = half
    blk = rows
    nb = width // blk
    side = lax.axis_index("cube")
    front_pos = lax.axis_index("front")
    col = lax.axis_index("col")
    row_block = lax.axis_index(("cube", "front"))
    row_start = row_block * rows
    col_start = col * width
    row_ids = row_start + jnp.arange(rows, dtype=jnp.int32)
    col_ids = col_start + jnp.arange(width, dtype=jnp.int32)

    own_map = lax.dynamic_index_in_dim(row_maps, side, 0, keepdims=False)
    other_map = lax.dynamic_index_in_dim(row_maps, 1 - side, 0, keepdims=False)
    first = front_pos * 2 * half + side * half
    own_rows = lax.dynamic_slice_in_dim(own_map, first, half) - row_start
    other_rows = lax.dynamic_slice_in_dim(other_map, first, half) - row_start
    blk_starts = col_start + blk * jnp.arange(nb, dtype=jnp.int32)[:, None]
    pair = 2 * grp
    parity = (col * nb * blk) // (lax.axis_size("front") * blk)
    own_cols = column_span(own_map, col, nb, grp).reshape(nb, pair) - blk_starts
    other_cols = column_span(other_map, col, nb, grp).reshape(nb, pair)
    other_cols = lax.dynamic_slice_in_dim(other_cols, parity * grp, grp, 1) - blk_starts

    local_block = child_blocks[0]
    kept_rows = lax.dynamic_slice_in_dim(local_block, side * half, half, 0)
    sent_rows = lax.dynamic_slice_in_dim(local_block, (1 - side) * half, half, 0)
    kept = column_span(kept_rows, col, nb, grp)
    sent_span = column_span(sent_rows, col, nb, grp)
    pick = one_hot(parity * grp + jnp.arange(grp, dtype=jnp.int32), pair, sent_span.dtype).T
    sent = jnp.concatenate(
        [
            jnp.dot(sent_span[:, j * pair : (j + 1) * pair], pick, preferred_element_type=jnp.float32)
            for j in range(nb)
        ],
        axis=1,
    ).astype(sent_span.dtype)
    arrived = swapped(sent, "cube", 0)

    pcols = NP * PW
    hb = pcols // blk
    nfront = lax.axis_size("front")
    head_primary = parent_front[:, : hb * blk] + place(
        kept[:, : hb * pair], own_rows, own_cols[:hb], rows, blk
    )
    partner_start = ((1 - side) * nfront + front_pos) * rows
    sent_rows_local = (
        lax.dynamic_slice_in_dim(own_map, front_pos * 2 * half + (1 - side) * half, half)
        - partner_start
    )
    head_secondary = place(sent_span[:, : hb * pair], sent_rows_local, own_cols[:hb], rows, blk)
    contribution = jnp.where(side == 0, head_primary, head_secondary)
    own_part = place(kept, own_rows, own_cols, rows, blk)
    other_part = place(arrived, other_rows, other_cols, rows, blk)
    first_child = jnp.where(side == 0, own_part, other_part)
    second_child = jnp.where(side == 0, other_part, own_part)
    matrix = parent_front + first_child
    matrix = matrix + second_child

    live_rows = row_ids < front_size[0]
    live_cols = col_ids < front_size[0]
    matrix = jnp.where(live_rows[:, None] & live_cols[None, :], matrix, 0.0)
    matrix = matrix + jnp.where(
        (row_ids[:, None] == col_ids[None, :]) & jnp.logical_not(live_rows)[:, None], 1.0, 0.0
    )

    head_local = matrix[:, :pcols]
    ncol = lax.axis_size("col")

    everyone = ("cube", "front", "col")
    ndev = lax.axis_size(everyone)
    nd = pcols // rows
    widths = [(b + 1) * PW for b in range(nd)]
    chunks = [rows * w // ndev for w in widths]
    send = jnp.concatenate(
        [
            jnp.where((front_pos == b) & (col == 0), contribution[:, : widths[b]], 0.0).reshape(
                ndev, chunks[b]
            )
            for b in range(nd)
        ],
        axis=1,
    )
    scattered = lax.all_to_all(send, everyone, 0, 0, tiled=True)
    offsets = [sum(chunks[:b]) for b in range(nd)]
    piece = jnp.concatenate(
        [
            scattered[b * ncol, offsets[b] : offsets[b] + chunks[b]]
            + scattered[(nfront + b) * ncol, offsets[b] : offsets[b] + chunks[b]]
            for b in range(nd)
        ]
    )
    spread_out = jnp.broadcast_to(piece[None], (ndev, sum(chunks)))
    gathered_top = lax.all_to_all(spread_out, everyone, 0, 0, tiled=True)
    lower_rows = [
        gathered_top[:, offsets[b] : offsets[b] + chunks[b]].reshape(rows, widths[b])
        for b in range(nd)
    ]
    top = jnp.concatenate(
        [
            jnp.concatenate(
                [lower_rows[b]] + [lower_rows[m][:, b * PW : (b + 1) * PW].T for m in range(b + 1, nd)],
                axis=1,
            )
            for b in range(nd)
        ],
        axis=0,
    )
    top_ids = jnp.arange(pcols, dtype=jnp.int32)
    top_live = top_ids < front_size[0]
    top = jnp.where(top_live[:, None] & top_live[None, :], top, 0.0)
    top = top + jnp.where(
        (top_ids[:, None] == top_ids[None, :]) & jnp.logical_not(top_live)[:, None], 1.0, 0.0
    )
    head_late, top = lax.optimization_barrier((head_local, top))
    arrived_heads = [lax.ppermute(head_late, "col", [(0, d)]) for d in range(1, ncol)]
    own = head_late
    for d, arrived_head in enumerate(arrived_heads, start=1):
        own = jnp.where(col == d, arrived_head, own)

    bw = PW // 2 if PW % 256 == 0 else PW
    nblk = pcols // bw
    eye = jnp.eye(bw, dtype=jnp.float32)
    trail = top
    diag_inverse = []
    low = {}
    for j in range(nblk):
        diag_factor = jnp.linalg.cholesky(trail[:bw, :bw])
        inverse = lax.linalg.triangular_solve(
            diag_factor, eye, left_side=True, lower=True, transpose_a=False
        )
        diag_inverse.append(inverse)
        if j == 0:
            own, inverse = lax.optimization_barrier((own, inverse))
            diag_inverse[0] = inverse
            col_head = lax.dynamic_slice_in_dim(
                lax.all_gather(own, ("cube", "front"), tiled=True), col_start, width, 0
            )
        if j + 1 < nblk:
            below = jnp.dot(trail[bw:, :bw], inverse.T, precision=HI)
            for i in range(j + 1, nblk):
                low[i, j] = below[(i - j - 1) * bw : (i - j) * bw]
            trail = trail[bw:, bw:] - jnp.dot(below, below.T, precision=HI)

    top_inverse = diag_inverse[0]
    for p in range(1, nblk):
        links = jnp.concatenate([low[p, m] for m in range(p)], axis=1)
        left = -jnp.dot(diag_inverse[p], jnp.dot(links, top_inverse, precision=HI), precision=HI)
        top_inverse = jnp.concatenate(
            [
                jnp.concatenate([top_inverse, jnp.zeros((p * bw, bw), jnp.float32)], axis=1),
                jnp.concatenate([left, diag_inverse[p]], axis=1),
            ],
            axis=0,
        )

    factor = jnp.dot(own, top_inverse.T, precision=HI)
    factor_cols = jnp.arange(pcols, dtype=jnp.int32)
    factor = jnp.where(row_ids[:, None] >= (factor_cols // PW * PW)[None, :], factor, 0.0)
    weights = jnp.dot(factor, top_inverse, precision=HI)
    update = lax.dot_general(weights, col_head, (((1,), (1,)), ((), ())), precision=HI)
    matrix = matrix - update
    keep_rows = row_ids >= K
    keep_cols = col_ids >= K
    schur = jnp.where(keep_rows[:, None] & keep_cols[None, :], matrix, 0.0)
    return (factor, schur)


def solution(mesh):
    in_specs = (P(("cube", "front"), "col"), P("cube", "front", None), P(), P())
    out_specs = (P(("cube", "front"), None), P(("cube", "front"), "col"))
    return jax.shard_map(shards, mesh=mesh, in_specs=in_specs, out_specs=out_specs, check_vma=False)
```

```python
import jax
import jax.numpy as jnp
from jax import lax
from jax.sharding import PartitionSpec as P

PW = 256
NP = 2
K = 512

HI = lax.Precision.HIGHEST


def swapped(shard, axis, distance):
    return lax.ppermute(shard, axis, [(i, i ^ 1 << distance) for i in range(lax.axis_size(axis))])


def spread(block, axis, owner):
    block = jnp.where(lax.axis_index(axis) == owner, block, jnp.zeros_like(block))
    return lax.psum(block, axis)


def column_span(block, col, nb, grp):
    span = nb * 2 * grp
    start = (col * span) % block.shape[-1]
    return lax.dynamic_slice_in_dim(block, start, span, block.ndim - 1)


def one_hot(index, size, dtype):
    return (index[..., None] == jnp.arange(size, dtype=jnp.int32)).astype(dtype)


def place(part, row_local, col_local, rows, blk):
    nb, w = col_local.shape
    pr = one_hot(row_local, rows, part.dtype).T
    placed_rows = jnp.dot(pr, part, preferred_element_type=jnp.float32).astype(part.dtype)
    pieces = [
        jnp.dot(
            placed_rows[:, j * w : (j + 1) * w],
            one_hot(col_local[j], blk, part.dtype),
            preferred_element_type=jnp.float32,
        )
        for j in range(nb)
    ]
    return jnp.concatenate(pieces, axis=1)


def shards(parent_front, child_blocks, row_maps, front_size):
    rows, width = parent_front.shape
    half = child_blocks.shape[1] // 2
    grp = half
    blk = rows
    nb = width // blk
    side = lax.axis_index("cube")
    front_pos = lax.axis_index("front")
    col = lax.axis_index("col")
    row_block = lax.axis_index(("cube", "front"))
    row_start = row_block * rows
    col_start = col * width
    row_ids = row_start + jnp.arange(rows, dtype=jnp.int32)
    col_ids = col_start + jnp.arange(width, dtype=jnp.int32)

    own_map = lax.dynamic_index_in_dim(row_maps, side, 0, keepdims=False)
    other_map = lax.dynamic_index_in_dim(row_maps, 1 - side, 0, keepdims=False)
    first = front_pos * 2 * half + side * half
    own_rows = lax.dynamic_slice_in_dim(own_map, first, half) - row_start
    other_rows = lax.dynamic_slice_in_dim(other_map, first, half) - row_start
    blk_starts = col_start + blk * jnp.arange(nb, dtype=jnp.int32)[:, None]
    pair = 2 * grp
    parity = (col * nb * blk) // (lax.axis_size("front") * blk)
    own_cols = column_span(own_map, col, nb, grp).reshape(nb, pair) - blk_starts
    other_cols = column_span(other_map, col, nb, grp).reshape(nb, pair)
    other_cols = lax.dynamic_slice_in_dim(other_cols, parity * grp, grp, 1) - blk_starts

    local_block = child_blocks[0]
    kept_rows = lax.dynamic_slice_in_dim(local_block, side * half, half, 0)
    sent_rows = lax.dynamic_slice_in_dim(local_block, (1 - side) * half, half, 0)
    kept = column_span(kept_rows, col, nb, grp)
    sent_span = column_span(sent_rows, col, nb, grp)
    pick = one_hot(parity * grp + jnp.arange(grp, dtype=jnp.int32), pair, sent_span.dtype).T
    sent = jnp.concatenate(
        [
            jnp.dot(sent_span[:, j * pair : (j + 1) * pair], pick, preferred_element_type=jnp.float32)
            for j in range(nb)
        ],
        axis=1,
    ).astype(sent_span.dtype)
    arrived = swapped(sent, "cube", 0)
    own_part = place(kept, own_rows, own_cols, rows, blk)
    other_part = place(arrived, other_rows, other_cols, rows, blk)
    first_child = jnp.where(side == 0, own_part, other_part)
    second_child = jnp.where(side == 0, other_part, own_part)
    matrix = parent_front + first_child
    matrix = matrix + second_child

    live_rows = row_ids < front_size[0]
    live_cols = col_ids < front_size[0]
    matrix = jnp.where(live_rows[:, None] & live_cols[None, :], matrix, 0.0)
    matrix = matrix + jnp.where(
        (row_ids[:, None] == col_ids[None, :]) & jnp.logical_not(live_rows)[:, None], 1.0, 0.0
    )

    pcols = NP * PW
    head_local = matrix[:, :pcols]
    ncol = lax.axis_size("col")

    everyone = ("cube", "front", "col")
    ndev = lax.axis_size(everyone)
    nd = pcols // rows
    widths = [(b + 1) * PW for b in range(nd)]
    chunks = [rows * w // ndev for w in widths]
    send = jnp.concatenate(
        [
            jnp.where((row_block == b) & (col == 0), head_local[:, : widths[b]], 0.0).reshape(
                ndev, chunks[b]
            )
            for b in range(nd)
        ],
        axis=1,
    )
    scattered = lax.all_to_all(send, everyone, 0, 0, tiled=True)
    head_late, scattered = lax.optimization_barrier((head_local, scattered))
    offsets = [sum(chunks[:b]) for b in range(nd)]
    piece = jnp.concatenate(
        [scattered[b * ncol, offsets[b] : offsets[b] + chunks[b]] for b in range(nd)]
    )
    spread_out = jnp.broadcast_to(piece[None], (ndev, sum(chunks)))
    gathered_top = lax.all_to_all(spread_out, everyone, 0, 0, tiled=True)
    lower_rows = [
        gathered_top[:, offsets[b] : offsets[b] + chunks[b]].reshape(rows, widths[b])
        for b in range(nd)
    ]
    top = jnp.concatenate(
        [
            jnp.concatenate(
                [lower_rows[b]] + [lower_rows[m][:, b * PW : (b + 1) * PW].T for m in range(b + 1, nd)],
                axis=1,
            )
            for b in range(nd)
        ],
        axis=0,
    )
    arrived_heads = [lax.ppermute(head_late, "col", [(0, d)]) for d in range(1, ncol)]
    own = head_late
    for d, arrived_head in enumerate(arrived_heads, start=1):
        own = jnp.where(col == d, arrived_head, own)

    bw = PW // 2 if PW % 256 == 0 else PW
    nblk = pcols // bw
    eye = jnp.eye(bw, dtype=jnp.float32)
    trail = top
    diag_inverse = []
    low = {}
    for j in range(nblk):
        diag_factor = jnp.linalg.cholesky(trail[:bw, :bw])
        inverse = lax.linalg.triangular_solve(
            diag_factor, eye, left_side=True, lower=True, transpose_a=False
        )
        diag_inverse.append(inverse)
        if j == 0:
            own, inverse = lax.optimization_barrier((own, inverse))
            diag_inverse[0] = inverse
            col_head = lax.dynamic_slice_in_dim(
                lax.all_gather(own, ("cube", "front"), tiled=True), col_start, width, 0
            )
        if j + 1 < nblk:
            below = jnp.dot(trail[bw:, :bw], inverse.T, precision=HI)
            for i in range(j + 1, nblk):
                low[i, j] = below[(i - j - 1) * bw : (i - j) * bw]
            trail = trail[bw:, bw:] - jnp.dot(below, below.T, precision=HI)

    top_inverse = diag_inverse[0]
    for p in range(1, nblk):
        links = jnp.concatenate([low[p, m] for m in range(p)], axis=1)
        left = -jnp.dot(diag_inverse[p], jnp.dot(links, top_inverse, precision=HI), precision=HI)
        top_inverse = jnp.concatenate(
            [
                jnp.concatenate([top_inverse, jnp.zeros((p * bw, bw), jnp.float32)], axis=1),
                jnp.concatenate([left, diag_inverse[p]], axis=1),
            ],
            axis=0,
        )

    factor = jnp.dot(own, top_inverse.T, precision=HI)
    factor_cols = jnp.arange(pcols, dtype=jnp.int32)
    factor = jnp.where(row_ids[:, None] >= (factor_cols // PW * PW)[None, :], factor, 0.0)
    weights = jnp.dot(factor, top_inverse, precision=HI)
    update = lax.dot_general(weights, col_head, (((1,), (1,)), ((), ())), precision=HI)
    matrix = matrix - update
    keep_rows = row_ids >= K
    keep_cols = col_ids >= K
    schur = jnp.where(keep_rows[:, None] & keep_cols[None, :], matrix, 0.0)
    return (factor, schur)


def solution(mesh):
    in_specs = (P(("cube", "front"), "col"), P("cube", "front", None), P(), P())
    out_specs = (P(("cube", "front"), None), P(("cube", "front"), "col"))
    return jax.shard_map(shards, mesh=mesh, in_specs=in_specs, out_specs=out_specs, check_vma=False)
```

```python
import jax
import jax.numpy as jnp
from jax import lax
from jax.sharding import PartitionSpec as P
from jax.experimental.layout import Layout, with_layout_constraint

PW = 256
NP = 2
K = 512

HI = lax.Precision.HIGHEST


def swapped(shard, axis, distance):
    return lax.ppermute(shard, axis, [(i, i ^ 1 << distance) for i in range(lax.axis_size(axis))])


def spread(block, axis, owner):
    block = jnp.where(lax.axis_index(axis) == owner, block, jnp.zeros_like(block))
    return lax.psum(block, axis)


def column_span(block, col, nb, grp):
    span = nb * 2 * grp
    start = (col * span) % block.shape[-1]
    return lax.dynamic_slice_in_dim(block, start, span, block.ndim - 1)


def one_hot(index, size, dtype):
    return (index[..., None] == jnp.arange(size, dtype=jnp.int32)).astype(dtype)


def place(part, row_local, col_local, rows, blk):
    nb, w = col_local.shape
    pr = one_hot(row_local, rows, part.dtype).T
    placed_rows = jnp.dot(pr, part, preferred_element_type=jnp.float32).astype(part.dtype)
    pieces = [
        jnp.dot(
            placed_rows[:, j * w : (j + 1) * w],
            one_hot(col_local[j], blk, part.dtype),
            preferred_element_type=jnp.float32,
        )
        for j in range(nb)
    ]
    return jnp.concatenate(pieces, axis=1)


def shards(parent_front, child_blocks, row_maps, front_size):
    rows, width = parent_front.shape
    half = child_blocks.shape[1] // 2
    grp = half
    blk = rows
    nb = width // blk
    side = lax.axis_index("cube")
    front_pos = lax.axis_index("front")
    col = lax.axis_index("col")
    row_block = lax.axis_index(("cube", "front"))
    row_start = row_block * rows
    col_start = col * width
    row_ids = row_start + jnp.arange(rows, dtype=jnp.int32)
    col_ids = col_start + jnp.arange(width, dtype=jnp.int32)

    own_map = lax.dynamic_index_in_dim(row_maps, side, 0, keepdims=False)
    other_map = lax.dynamic_index_in_dim(row_maps, 1 - side, 0, keepdims=False)
    first = front_pos * 2 * half + side * half
    own_rows = lax.dynamic_slice_in_dim(own_map, first, half) - row_start
    other_rows = lax.dynamic_slice_in_dim(other_map, first, half) - row_start
    blk_starts = col_start + blk * jnp.arange(nb, dtype=jnp.int32)[:, None]
    pair = 2 * grp
    parity = (col * nb * blk) // (lax.axis_size("front") * blk)
    own_cols = column_span(own_map, col, nb, grp).reshape(nb, pair) - blk_starts
    other_cols = column_span(other_map, col, nb, grp).reshape(nb, pair)
    other_cols = lax.dynamic_slice_in_dim(other_cols, parity * grp, grp, 1) - blk_starts

    local_block = child_blocks[0]
    kept_rows = lax.dynamic_slice_in_dim(local_block, side * half, half, 0)
    sent_rows = lax.dynamic_slice_in_dim(local_block, (1 - side) * half, half, 0)
    kept = column_span(kept_rows, col, nb, grp)
    sent_span = column_span(sent_rows, col, nb, grp)
    pick = one_hot(parity * grp + jnp.arange(grp, dtype=jnp.int32), pair, sent_span.dtype).T
    sent = jnp.concatenate(
        [
            jnp.dot(sent_span[:, j * pair : (j + 1) * pair], pick, preferred_element_type=jnp.float32)
            for j in range(nb)
        ],
        axis=1,
    ).astype(sent_span.dtype)
    arrived = swapped(sent, "cube", 0)
    own_part = place(kept, own_rows, own_cols, rows, blk)
    other_part = place(arrived, other_rows, other_cols, rows, blk)
    first_child = jnp.where(side == 0, own_part, other_part)
    second_child = jnp.where(side == 0, other_part, own_part)
    matrix = parent_front + first_child
    matrix = matrix + second_child

    live_rows = row_ids < front_size[0]
    live_cols = col_ids < front_size[0]
    matrix = jnp.where(live_rows[:, None] & live_cols[None, :], matrix, 0.0)
    matrix = matrix + jnp.where(
        (row_ids[:, None] == col_ids[None, :]) & jnp.logical_not(live_rows)[:, None], 1.0, 0.0
    )
    matrix = with_layout_constraint(matrix, Layout(major_to_minor=(0, 1)))

    pcols = NP * PW
    head_local = matrix[:, :pcols]
    ncol = lax.axis_size("col")

    everyone = ("cube", "front", "col")
    ndev = lax.axis_size(everyone)
    nd = pcols // rows
    widths = [(b + 1) * PW for b in range(nd)]
    chunks = [rows * w // ndev for w in widths]
    send = jnp.concatenate(
        [
            jnp.where((row_block == b) & (col == 0), head_local[:, : widths[b]], 0.0).reshape(
                ndev, chunks[b]
            )
            for b in range(nd)
        ],
        axis=1,
    )
    scattered = lax.all_to_all(send, everyone, 0, 0, tiled=True)
    head_late, scattered = lax.optimization_barrier((head_local, scattered))
    offsets = [sum(chunks[:b]) for b in range(nd)]
    piece = jnp.concatenate(
        [scattered[b * ncol, offsets[b] : offsets[b] + chunks[b]] for b in range(nd)]
    )
    spread_out = jnp.broadcast_to(piece[None], (ndev, sum(chunks)))
    gathered_top = lax.all_to_all(spread_out, everyone, 0, 0, tiled=True)
    lower_rows = [
        gathered_top[:, offsets[b] : offsets[b] + chunks[b]].reshape(rows, widths[b])
        for b in range(nd)
    ]
    top = jnp.concatenate(
        [
            jnp.concatenate(
                [lower_rows[b]] + [lower_rows[m][:, b * PW : (b + 1) * PW].T for m in range(b + 1, nd)],
                axis=1,
            )
            for b in range(nd)
        ],
        axis=0,
    )
    arrived_heads = [lax.ppermute(head_late, "col", [(0, d)]) for d in range(1, ncol)]
    own = head_late
    for d, arrived_head in enumerate(arrived_heads, start=1):
        own = jnp.where(col == d, arrived_head, own)

    bw = PW // 2 if PW % 256 == 0 else PW
    nblk = pcols // bw
    eye = jnp.eye(bw, dtype=jnp.float32)
    trail = top
    diag_inverse = []
    low = {}
    for j in range(nblk):
        diag_factor = jnp.linalg.cholesky(trail[:bw, :bw])
        inverse = lax.linalg.triangular_solve(
            diag_factor, eye, left_side=True, lower=True, transpose_a=False
        )
        diag_inverse.append(inverse)
        if j == 0:
            own, inverse = lax.optimization_barrier((own, inverse))
            diag_inverse[0] = inverse
            col_head = lax.dynamic_slice_in_dim(
                lax.all_gather(own, ("cube", "front"), tiled=True), col_start, width, 0
            )
        if j + 1 < nblk:
            below = jnp.dot(trail[bw:, :bw], inverse.T, precision=HI)
            for i in range(j + 1, nblk):
                low[i, j] = below[(i - j - 1) * bw : (i - j) * bw]
            trail = trail[bw:, bw:] - jnp.dot(below, below.T, precision=HI)

    top_inverse = diag_inverse[0]
    for p in range(1, nblk):
        links = jnp.concatenate([low[p, m] for m in range(p)], axis=1)
        left = -jnp.dot(diag_inverse[p], jnp.dot(links, top_inverse, precision=HI), precision=HI)
        top_inverse = jnp.concatenate(
            [
                jnp.concatenate([top_inverse, jnp.zeros((p * bw, bw), jnp.float32)], axis=1),
                jnp.concatenate([left, diag_inverse[p]], axis=1),
            ],
            axis=0,
        )

    factor = jnp.dot(own, top_inverse.T, precision=HI)
    factor_cols = jnp.arange(pcols, dtype=jnp.int32)
    factor = jnp.where(row_ids[:, None] >= (factor_cols // PW * PW)[None, :], factor, 0.0)
    weights = jnp.dot(factor, top_inverse, precision=HI)
    update = lax.dot_general(weights, col_head, (((1,), (1,)), ((), ())), precision=HI)
    matrix = matrix - update
    keep_rows = row_ids >= K
    keep_cols = col_ids >= K
    schur = jnp.where(keep_rows[:, None] & keep_cols[None, :], matrix, 0.0)
    return (factor, schur)


def solution(mesh):
    in_specs = (P(("cube", "front"), "col"), P("cube", "front", None), P(), P())
    out_specs = (P(("cube", "front"), None), P(("cube", "front"), "col"))
    return jax.shard_map(shards, mesh=mesh, in_specs=in_specs, out_specs=out_specs, check_vma=False)
```

```python
import jax
import jax.numpy as jnp
from jax import lax
from jax.sharding import PartitionSpec as P
from jax.experimental.layout import Layout, with_layout_constraint

PW = 256
NP = 2
K = 512

HI = lax.Precision.HIGHEST


def swapped(shard, axis, distance):
    return lax.ppermute(shard, axis, [(i, i ^ 1 << distance) for i in range(lax.axis_size(axis))])


def column_span(block, col, nb, grp):
    span = nb * 2 * grp
    start = (col * span) % block.shape[-1]
    return lax.dynamic_slice_in_dim(block, start, span, block.ndim - 1)


def one_hot(index, size, dtype):
    return (index[..., None] == jnp.arange(size, dtype=jnp.int32)).astype(dtype)


def place(part, row_local, col_local, rows, blk):
    nb, w = col_local.shape
    pr = one_hot(row_local, rows, part.dtype).T
    placed_rows = jnp.dot(pr, part, preferred_element_type=jnp.float32).astype(part.dtype)
    pieces = [
        jnp.dot(
            placed_rows[:, j * w : (j + 1) * w],
            one_hot(col_local[j], blk, part.dtype),
            preferred_element_type=jnp.float32,
        )
        for j in range(nb)
    ]
    return jnp.concatenate(pieces, axis=1)


def shards(parent_front, child_blocks, row_maps, front_size):
    rows, width = parent_front.shape
    half = child_blocks.shape[1] // 2
    grp = half
    blk = rows
    nb = width // blk
    side = lax.axis_index("cube")
    front_pos = lax.axis_index("front")
    col = lax.axis_index("col")
    row_block = lax.axis_index(("cube", "front"))
    row_start = row_block * rows
    col_start = col * width
    row_ids = row_start + jnp.arange(rows, dtype=jnp.int32)
    col_ids = col_start + jnp.arange(width, dtype=jnp.int32)

    own_map = lax.dynamic_index_in_dim(row_maps, side, 0, keepdims=False)
    other_map = lax.dynamic_index_in_dim(row_maps, 1 - side, 0, keepdims=False)
    first = front_pos * 2 * half + side * half
    own_rows = lax.dynamic_slice_in_dim(own_map, first, half) - row_start
    other_rows = lax.dynamic_slice_in_dim(other_map, first, half) - row_start
    blk_starts = col_start + blk * jnp.arange(nb, dtype=jnp.int32)[:, None]
    pair = 2 * grp
    parity = (col * nb * blk) // (lax.axis_size("front") * blk)
    own_cols = column_span(own_map, col, nb, grp).reshape(nb, pair) - blk_starts
    other_cols = column_span(other_map, col, nb, grp).reshape(nb, pair)
    other_cols = lax.dynamic_slice_in_dim(other_cols, parity * grp, grp, 1) - blk_starts

    local_block = child_blocks[0]
    kept_rows = lax.dynamic_slice_in_dim(local_block, side * half, half, 0)
    sent_rows = lax.dynamic_slice_in_dim(local_block, (1 - side) * half, half, 0)
    kept = column_span(kept_rows, col, nb, grp)
    sent_span = column_span(sent_rows, col, nb, grp)
    pick = one_hot(parity * grp + jnp.arange(grp, dtype=jnp.int32), pair, sent_span.dtype).T
    sent = jnp.concatenate(
        [
            jnp.dot(sent_span[:, j * pair : (j + 1) * pair], pick, preferred_element_type=jnp.float32)
            for j in range(nb)
        ],
        axis=1,
    ).astype(sent_span.dtype)
    arrived = swapped(sent, "cube", 0)
    pcols = NP * PW
    hb = pcols // blk
    live_rows = row_ids < front_size[0]

    def assemble(lo, hi):
        span = slice(lo * blk, hi * blk)
        own_part = place(kept[:, lo * pair : hi * pair], own_rows, own_cols[lo:hi], rows, blk)
        other_part = place(arrived[:, lo * grp : hi * grp], other_rows, other_cols[lo:hi], rows, blk)
        first_child = jnp.where(side == 0, own_part, other_part)
        second_child = jnp.where(side == 0, other_part, own_part)
        part = parent_front[:, span] + first_child
        part = part + second_child
        ids = col_ids[span]
        live_cols = ids < front_size[0]
        part = jnp.where(live_rows[:, None] & live_cols[None, :], part, 0.0)
        part = part + jnp.where(
            (row_ids[:, None] == ids[None, :]) & jnp.logical_not(live_rows)[:, None], 1.0, 0.0
        )
        return with_layout_constraint(part, Layout(major_to_minor=(0, 1)))

    head_local = assemble(0, hb)
    rest = assemble(hb, nb)

    ncol = lax.axis_size("col")

    everyone = ("cube", "front", "col")
    ndev = lax.axis_size(everyone)
    nd = pcols // rows
    widths = [(b + 1) * PW for b in range(nd)]
    chunks = [rows * w // ndev for w in widths]
    send = jnp.concatenate(
        [
            jnp.where((row_block == b) & (col == 0), head_local[:, : widths[b]], 0.0).reshape(
                ndev, chunks[b]
            )
            for b in range(nd)
        ],
        axis=1,
    )
    scattered = lax.all_to_all(send, everyone, 0, 0, tiled=True)
    head_late, scattered = lax.optimization_barrier((head_local, scattered))
    offsets = [sum(chunks[:b]) for b in range(nd)]
    piece = jnp.concatenate(
        [scattered[b * ncol, offsets[b] : offsets[b] + chunks[b]] for b in range(nd)]
    )
    spread_out = jnp.broadcast_to(piece[None], (ndev, sum(chunks)))
    gathered_top = lax.all_to_all(spread_out, everyone, 0, 0, tiled=True)
    lower_rows = [
        gathered_top[:, offsets[b] : offsets[b] + chunks[b]].reshape(rows, widths[b])
        for b in range(nd)
    ]
    top = jnp.concatenate(
        [
            jnp.concatenate(
                [lower_rows[b]] + [lower_rows[m][:, b * PW : (b + 1) * PW].T for m in range(b + 1, nd)],
                axis=1,
            )
            for b in range(nd)
        ],
        axis=0,
    )
    arrived_heads = [lax.ppermute(head_late, "col", [(0, d)]) for d in range(1, ncol)]
    own = head_late
    for d, arrived_head in enumerate(arrived_heads, start=1):
        own = jnp.where(col == d, arrived_head, own)

    bw = PW // 2 if PW % 256 == 0 else PW
    nblk = pcols // bw
    eye = jnp.eye(bw, dtype=jnp.float32)
    trail = top
    diag_inverse = []
    low = {}
    for j in range(nblk):
        diag_factor = jnp.linalg.cholesky(trail[:bw, :bw])
        inverse = lax.linalg.triangular_solve(
            diag_factor, eye, left_side=True, lower=True, transpose_a=False
        )
        diag_inverse.append(inverse)
        if j == 0:
            own, inverse = lax.optimization_barrier((own, inverse))
            diag_inverse[0] = inverse
            col_head = lax.dynamic_slice_in_dim(
                lax.all_gather(own, ("cube", "front"), tiled=True), col_start, width, 0
            )
        if j + 1 < nblk:
            below = jnp.dot(trail[bw:, :bw], inverse.T, precision=HI)
            for i in range(j + 1, nblk):
                low[i, j] = below[(i - j - 1) * bw : (i - j) * bw]
            trail = trail[bw:, bw:] - jnp.dot(below, below.T, precision=HI)

    top_inverse = diag_inverse[0]
    for p in range(1, nblk):
        links = jnp.concatenate([low[p, m] for m in range(p)], axis=1)
        left = -jnp.dot(diag_inverse[p], jnp.dot(links, top_inverse, precision=HI), precision=HI)
        top_inverse = jnp.concatenate(
            [
                jnp.concatenate([top_inverse, jnp.zeros((p * bw, bw), jnp.float32)], axis=1),
                jnp.concatenate([left, diag_inverse[p]], axis=1),
            ],
            axis=0,
        )

    factor = jnp.dot(own, top_inverse.T, precision=HI)
    factor_cols = jnp.arange(pcols, dtype=jnp.int32)
    factor = jnp.where(row_ids[:, None] >= (factor_cols // PW * PW)[None, :], factor, 0.0)
    weights = jnp.dot(factor, top_inverse, precision=HI)
    update = lax.dot_general(weights, col_head, (((1,), (1,)), ((), ())), precision=HI)
    matrix = jnp.concatenate([head_local, rest], axis=1) - update
    keep_rows = row_ids >= K
    keep_cols = col_ids >= K
    schur = jnp.where(keep_rows[:, None] & keep_cols[None, :], matrix, 0.0)
    return (factor, schur)


def solution(mesh):
    in_specs = (P(("cube", "front"), "col"), P("cube", "front", None), P(), P())
    out_specs = (P(("cube", "front"), None), P(("cube", "front"), "col"))
    return jax.shard_map(shards, mesh=mesh, in_specs=in_specs, out_specs=out_specs, check_vma=False)
```

```python
import jax
import jax.numpy as jnp
from jax import lax
from jax.sharding import PartitionSpec as P
from jax.experimental.layout import Layout, with_layout_constraint

PW = 256
NP = 2
K = 512

HI = lax.Precision.HIGHEST


def swapped(shard, axis, distance):
    return lax.ppermute(shard, axis, [(i, i ^ 1 << distance) for i in range(lax.axis_size(axis))])


def column_span(block, col, nb, grp):
    span = nb * 2 * grp
    start = (col * span) % block.shape[-1]
    return lax.dynamic_slice_in_dim(block, start, span, block.ndim - 1)


def one_hot(index, size, dtype):
    return (index[..., None] == jnp.arange(size, dtype=jnp.int32)).astype(dtype)


def place(part, row_local, col_local, rows, blk):
    nb, w = col_local.shape
    pr = one_hot(row_local, rows, part.dtype).T
    placed_rows = jnp.dot(pr, part, preferred_element_type=jnp.float32).astype(part.dtype)
    pieces = [
        jnp.dot(
            placed_rows[:, j * w : (j + 1) * w],
            one_hot(col_local[j], blk, part.dtype),
            preferred_element_type=jnp.float32,
        )
        for j in range(nb)
    ]
    return jnp.concatenate(pieces, axis=1)


def shards(parent_front, child_blocks, row_maps, front_size):
    rows, width = parent_front.shape
    half = child_blocks.shape[1] // 2
    grp = half
    blk = rows
    nb = width // blk
    side = lax.axis_index("cube")
    front_pos = lax.axis_index("front")
    col = lax.axis_index("col")
    row_block = lax.axis_index(("cube", "front"))
    row_start = row_block * rows
    col_start = col * width
    row_ids = row_start + jnp.arange(rows, dtype=jnp.int32)
    col_ids = col_start + jnp.arange(width, dtype=jnp.int32)

    own_map = lax.dynamic_index_in_dim(row_maps, side, 0, keepdims=False)
    other_map = lax.dynamic_index_in_dim(row_maps, 1 - side, 0, keepdims=False)
    first = front_pos * 2 * half + side * half
    own_rows = lax.dynamic_slice_in_dim(own_map, first, half) - row_start
    other_rows = lax.dynamic_slice_in_dim(other_map, first, half) - row_start
    blk_starts = col_start + blk * jnp.arange(nb, dtype=jnp.int32)[:, None]
    pair = 2 * grp
    parity = (col * nb * blk) // (lax.axis_size("front") * blk)
    own_cols = column_span(own_map, col, nb, grp).reshape(nb, pair) - blk_starts
    other_cols = column_span(other_map, col, nb, grp).reshape(nb, pair)
    other_cols = lax.dynamic_slice_in_dim(other_cols, parity * grp, grp, 1) - blk_starts

    local_block = child_blocks[0]
    kept_rows = lax.dynamic_slice_in_dim(local_block, side * half, half, 0)
    sent_rows = lax.dynamic_slice_in_dim(local_block, (1 - side) * half, half, 0)
    kept = column_span(kept_rows, col, nb, grp)
    sent_span = column_span(sent_rows, col, nb, grp)
    pick = one_hot(parity * grp + jnp.arange(grp, dtype=jnp.int32), pair, sent_span.dtype).T
    sent = jnp.concatenate(
        [
            jnp.dot(sent_span[:, j * pair : (j + 1) * pair], pick, preferred_element_type=jnp.float32)
            for j in range(nb)
        ],
        axis=1,
    ).astype(sent_span.dtype)
    pcols = NP * PW
    hb = pcols // blk
    live_rows = row_ids < front_size[0]

    arrived_head = swapped(sent[:, : hb * grp], "cube", 0)
    arrived_rest = swapped(sent[:, hb * grp :], "cube", 0)

    def assemble(lo, hi, arrived_part):
        span = slice(lo * blk, hi * blk)
        own_part = place(kept[:, lo * pair : hi * pair], own_rows, own_cols[lo:hi], rows, blk)
        other_part = place(arrived_part, other_rows, other_cols[lo:hi], rows, blk)
        first_child = jnp.where(side == 0, own_part, other_part)
        second_child = jnp.where(side == 0, other_part, own_part)
        part = parent_front[:, span] + first_child
        part = part + second_child
        ids = col_ids[span]
        live_cols = ids < front_size[0]
        part = jnp.where(live_rows[:, None] & live_cols[None, :], part, 0.0)
        part = part + jnp.where(
            (row_ids[:, None] == ids[None, :]) & jnp.logical_not(live_rows)[:, None], 1.0, 0.0
        )
        return with_layout_constraint(part, Layout(major_to_minor=(0, 1)))

    head_local = assemble(0, hb, arrived_head)
    rest = assemble(hb, nb, arrived_rest)

    ncol = lax.axis_size("col")

    everyone = ("cube", "front", "col")
    ndev = lax.axis_size(everyone)
    nd = pcols // rows
    widths = [(b + 1) * PW for b in range(nd)]
    chunks = [rows * w // ndev for w in widths]
    send = jnp.concatenate(
        [
            jnp.where((row_block == b) & (col == 0), head_local[:, : widths[b]], 0.0).reshape(
                ndev, chunks[b]
            )
            for b in range(nd)
        ],
        axis=1,
    )
    scattered = lax.all_to_all(send, everyone, 0, 0, tiled=True)
    head_late, scattered = lax.optimization_barrier((head_local, scattered))
    offsets = [sum(chunks[:b]) for b in range(nd)]
    piece = jnp.concatenate(
        [scattered[b * ncol, offsets[b] : offsets[b] + chunks[b]] for b in range(nd)]
    )
    spread_out = jnp.broadcast_to(piece[None], (ndev, sum(chunks)))
    gathered_top = lax.all_to_all(spread_out, everyone, 0, 0, tiled=True)
    lower_rows = [
        gathered_top[:, offsets[b] : offsets[b] + chunks[b]].reshape(rows, widths[b])
        for b in range(nd)
    ]
    top = jnp.concatenate(
        [
            jnp.concatenate(
                [lower_rows[b]] + [lower_rows[m][:, b * PW : (b + 1) * PW].T for m in range(b + 1, nd)],
                axis=1,
            )
            for b in range(nd)
        ],
        axis=0,
    )
    arrived_heads = [lax.ppermute(head_late, "col", [(0, d)]) for d in range(1, ncol)]
    own = head_late
    for d, arrived_head in enumerate(arrived_heads, start=1):
        own = jnp.where(col == d, arrived_head, own)

    bw = PW // 2 if PW % 256 == 0 else PW
    nblk = pcols // bw
    eye = jnp.eye(bw, dtype=jnp.float32)
    trail = top
    diag_inverse = []
    low = {}
    for j in range(nblk):
        diag_factor = jnp.linalg.cholesky(trail[:bw, :bw])
        inverse = lax.linalg.triangular_solve(
            diag_factor, eye, left_side=True, lower=True, transpose_a=False
        )
        diag_inverse.append(inverse)
        if j == 0:
            own, inverse = lax.optimization_barrier((own, inverse))
            diag_inverse[0] = inverse
            col_head = lax.dynamic_slice_in_dim(
                lax.all_gather(own, ("cube", "front"), tiled=True), col_start, width, 0
            )
        if j + 1 < nblk:
            below = jnp.dot(trail[bw:, :bw], inverse.T, precision=HI)
            for i in range(j + 1, nblk):
                low[i, j] = below[(i - j - 1) * bw : (i - j) * bw]
            trail = trail[bw:, bw:] - jnp.dot(below, below.T, precision=HI)

    top_inverse = diag_inverse[0]
    for p in range(1, nblk):
        links = jnp.concatenate([low[p, m] for m in range(p)], axis=1)
        left = -jnp.dot(diag_inverse[p], jnp.dot(links, top_inverse, precision=HI), precision=HI)
        top_inverse = jnp.concatenate(
            [
                jnp.concatenate([top_inverse, jnp.zeros((p * bw, bw), jnp.float32)], axis=1),
                jnp.concatenate([left, diag_inverse[p]], axis=1),
            ],
            axis=0,
        )

    factor = jnp.dot(own, top_inverse.T, precision=HI)
    factor_cols = jnp.arange(pcols, dtype=jnp.int32)
    factor = jnp.where(row_ids[:, None] >= (factor_cols // PW * PW)[None, :], factor, 0.0)
    weights = jnp.dot(factor, top_inverse, precision=HI)
    update = lax.dot_general(weights, col_head, (((1,), (1,)), ((), ())), precision=HI)
    matrix = jnp.concatenate([head_local, rest], axis=1) - update
    keep_rows = row_ids >= K
    keep_cols = col_ids >= K
    schur = jnp.where(keep_rows[:, None] & keep_cols[None, :], matrix, 0.0)
    return (factor, schur)


def solution(mesh):
    in_specs = (P(("cube", "front"), "col"), P("cube", "front", None), P(), P())
    out_specs = (P(("cube", "front"), None), P(("cube", "front"), "col"))
    return jax.shard_map(shards, mesh=mesh, in_specs=in_specs, out_specs=out_specs, check_vma=False)
```

```python
import jax
import jax.numpy as jnp
from jax import lax
from jax.sharding import PartitionSpec as P
from jax.experimental.layout import Layout, with_layout_constraint

PW = 256
NP = 2
K = 512

HI = lax.Precision.HIGHEST


def swapped(shard, axis, distance):
    return lax.ppermute(shard, axis, [(i, i ^ 1 << distance) for i in range(lax.axis_size(axis))])


def column_span(block, col, nb, grp):
    span = nb * 2 * grp
    start = (col * span) % block.shape[-1]
    return lax.dynamic_slice_in_dim(block, start, span, block.ndim - 1)


def one_hot(index, size, dtype):
    return (index[..., None] == jnp.arange(size, dtype=jnp.int32)).astype(dtype)


def place(part, row_local, col_local, rows, blk):
    nb, w = col_local.shape
    pr = one_hot(row_local, rows, part.dtype).T
    placed_rows = jnp.dot(pr, part, preferred_element_type=jnp.float32).astype(part.dtype)
    pieces = [
        jnp.dot(
            placed_rows[:, j * w : (j + 1) * w],
            one_hot(col_local[j], blk, part.dtype),
            preferred_element_type=jnp.float32,
        )
        for j in range(nb)
    ]
    return jnp.concatenate(pieces, axis=1)


def shards(parent_front, child_blocks, row_maps, front_size):
    rows, width = parent_front.shape
    half = child_blocks.shape[1] // 2
    grp = half
    blk = rows
    nb = width // blk
    side = lax.axis_index("cube")
    front_pos = lax.axis_index("front")
    col = lax.axis_index("col")
    row_block = lax.axis_index(("cube", "front"))
    row_start = row_block * rows
    col_start = col * width
    row_ids = row_start + jnp.arange(rows, dtype=jnp.int32)
    col_ids = col_start + jnp.arange(width, dtype=jnp.int32)

    own_map = lax.dynamic_index_in_dim(row_maps, side, 0, keepdims=False)
    other_map = lax.dynamic_index_in_dim(row_maps, 1 - side, 0, keepdims=False)
    first = front_pos * 2 * half + side * half
    own_rows = lax.dynamic_slice_in_dim(own_map, first, half) - row_start
    other_rows = lax.dynamic_slice_in_dim(other_map, first, half) - row_start
    blk_starts = col_start + blk * jnp.arange(nb, dtype=jnp.int32)[:, None]
    pair = 2 * grp
    parity = (col * nb * blk) // (lax.axis_size("front") * blk)
    own_cols = column_span(own_map, col, nb, grp).reshape(nb, pair) - blk_starts
    other_cols = column_span(other_map, col, nb, grp).reshape(nb, pair)
    other_cols = lax.dynamic_slice_in_dim(other_cols, parity * grp, grp, 1) - blk_starts

    local_block = child_blocks[0]
    kept_rows = lax.dynamic_slice_in_dim(local_block, side * half, half, 0)
    sent_rows = lax.dynamic_slice_in_dim(local_block, (1 - side) * half, half, 0)
    kept = column_span(kept_rows, col, nb, grp)
    sent_span = column_span(sent_rows, col, nb, grp)
    pick = one_hot(parity * grp + jnp.arange(grp, dtype=jnp.int32), pair, sent_span.dtype).T
    sent = jnp.concatenate(
        [
            jnp.dot(sent_span[:, j * pair : (j + 1) * pair], pick, preferred_element_type=jnp.float32)
            for j in range(nb)
        ],
        axis=1,
    ).astype(sent_span.dtype)
    pcols = NP * PW
    hb = pcols // blk
    live_rows = row_ids < front_size[0]

    arrived_head = swapped(sent[:, : hb * grp], "cube", 0)
    arrived_rest = swapped(sent[:, hb * grp :], "cube", 0)

    def assemble(lo, hi, arrived_part):
        span = slice(lo * blk, hi * blk)
        own_part = place(kept[:, lo * pair : hi * pair], own_rows, own_cols[lo:hi], rows, blk)
        other_part = place(arrived_part, other_rows, other_cols[lo:hi], rows, blk)
        first_child = jnp.where(side == 0, own_part, other_part)
        second_child = jnp.where(side == 0, other_part, own_part)
        part = parent_front[:, span] + first_child
        part = part + second_child
        ids = col_ids[span]
        live_cols = ids < front_size[0]
        part = jnp.where(live_rows[:, None] & live_cols[None, :], part, 0.0)
        part = part + jnp.where(
            (row_ids[:, None] == ids[None, :]) & jnp.logical_not(live_rows)[:, None], 1.0, 0.0
        )
        return with_layout_constraint(part, Layout(major_to_minor=(0, 1)))

    head_local = assemble(0, hb, arrived_head)
    nfront = lax.axis_size("front")
    head_primary = parent_front[:, : hb * blk] + place(
        kept[:, : hb * pair], own_rows, own_cols[:hb], rows, blk
    )
    partner_start = ((1 - side) * nfront + front_pos) * rows
    sent_rows_local = (
        lax.dynamic_slice_in_dim(own_map, front_pos * 2 * half + (1 - side) * half, half)
        - partner_start
    )
    head_secondary = place(sent_span[:, : hb * pair], sent_rows_local, own_cols[:hb], rows, blk)
    contribution = jnp.where(side == 0, head_primary, head_secondary)
    rest = assemble(hb, nb, arrived_rest)

    ncol = lax.axis_size("col")

    everyone = ("cube", "front", "col")
    ndev = lax.axis_size(everyone)
    nd = pcols // rows
    widths = [(b + 1) * PW for b in range(nd)]
    chunks = [rows * w // ndev for w in widths]
    send = jnp.concatenate(
        [
            jnp.where((front_pos == b) & (col == 0), contribution[:, : widths[b]], 0.0).reshape(
                ndev, chunks[b]
            )
            for b in range(nd)
        ],
        axis=1,
    )
    scattered = lax.all_to_all(send, everyone, 0, 0, tiled=True)
    head_late, scattered = lax.optimization_barrier((head_local, scattered))
    offsets = [sum(chunks[:b]) for b in range(nd)]
    piece = jnp.concatenate(
        [
            scattered[b * ncol, offsets[b] : offsets[b] + chunks[b]]
            + scattered[(nfront + b) * ncol, offsets[b] : offsets[b] + chunks[b]]
            for b in range(nd)
        ]
    )
    spread_out = jnp.broadcast_to(piece[None], (ndev, sum(chunks)))
    gathered_top = lax.all_to_all(spread_out, everyone, 0, 0, tiled=True)
    lower_rows = [
        gathered_top[:, offsets[b] : offsets[b] + chunks[b]].reshape(rows, widths[b])
        for b in range(nd)
    ]
    top = jnp.concatenate(
        [
            jnp.concatenate(
                [lower_rows[b]] + [lower_rows[m][:, b * PW : (b + 1) * PW].T for m in range(b + 1, nd)],
                axis=1,
            )
            for b in range(nd)
        ],
        axis=0,
    )
    top_ids = jnp.arange(pcols, dtype=jnp.int32)
    top_live = top_ids < front_size[0]
    top = jnp.where(top_live[:, None] & top_live[None, :], top, 0.0)
    top = top + jnp.where(
        (top_ids[:, None] == top_ids[None, :]) & jnp.logical_not(top_live)[:, None], 1.0, 0.0
    )
    arrived_heads = [lax.ppermute(head_late, "col", [(0, d)]) for d in range(1, ncol)]
    own = head_late
    for d, arrived_head in enumerate(arrived_heads, start=1):
        own = jnp.where(col == d, arrived_head, own)

    bw = PW // 2 if PW % 256 == 0 else PW
    nblk = pcols // bw
    eye = jnp.eye(bw, dtype=jnp.float32)
    trail = top
    diag_inverse = []
    low = {}
    for j in range(nblk):
        diag_factor = jnp.linalg.cholesky(trail[:bw, :bw])
        inverse = lax.linalg.triangular_solve(
            diag_factor, eye, left_side=True, lower=True, transpose_a=False
        )
        diag_inverse.append(inverse)
        if j == 0:
            own, inverse = lax.optimization_barrier((own, inverse))
            diag_inverse[0] = inverse
            col_head = lax.dynamic_slice_in_dim(
                lax.all_gather(own, ("cube", "front"), tiled=True), col_start, width, 0
            )
        if j + 1 < nblk:
            below = jnp.dot(trail[bw:, :bw], inverse.T, precision=HI)
            for i in range(j + 1, nblk):
                low[i, j] = below[(i - j - 1) * bw : (i - j) * bw]
            trail = trail[bw:, bw:] - jnp.dot(below, below.T, precision=HI)

    top_inverse = diag_inverse[0]
    for p in range(1, nblk):
        links = jnp.concatenate([low[p, m] for m in range(p)], axis=1)
        left = -jnp.dot(diag_inverse[p], jnp.dot(links, top_inverse, precision=HI), precision=HI)
        top_inverse = jnp.concatenate(
            [
                jnp.concatenate([top_inverse, jnp.zeros((p * bw, bw), jnp.float32)], axis=1),
                jnp.concatenate([left, diag_inverse[p]], axis=1),
            ],
            axis=0,
        )

    factor = jnp.dot(own, top_inverse.T, precision=HI)
    factor_cols = jnp.arange(pcols, dtype=jnp.int32)
    factor = jnp.where(row_ids[:, None] >= (factor_cols // PW * PW)[None, :], factor, 0.0)
    weights = jnp.dot(factor, top_inverse, precision=HI)
    update = lax.dot_general(weights, col_head, (((1,), (1,)), ((), ())), precision=HI)
    matrix = jnp.concatenate([head_local, rest], axis=1) - update
    keep_rows = row_ids >= K
    keep_cols = col_ids >= K
    schur = jnp.where(keep_rows[:, None] & keep_cols[None, :], matrix, 0.0)
    return (factor, schur)


def solution(mesh):
    in_specs = (P(("cube", "front"), "col"), P("cube", "front", None), P(), P())
    out_specs = (P(("cube", "front"), None), P(("cube", "front"), "col"))
    return jax.shard_map(shards, mesh=mesh, in_specs=in_specs, out_specs=out_specs, check_vma=False)
```
